768 devices in a mesh: energy: 48 (over z_hi, y, core), layer: 16 (over z_lo, x).
Axes of the slice: x: 4, y: 8, z: 12 (z_hi: 3, z_lo: 4; z = z_hi * 4 + z_lo), core: 2. Of those that a mesh axis runs over, the one named last changes fastest.
Arguments:
- retarded: bfloat16 [48, 48, 3, 256, 256], P('energy', 'layer'), may hold values from -0.375 to 0.375
- scatter_in: bfloat16 [48, 48, 256, 256], P('energy', 'layer'), may hold values from -6 to 6
- screen: bfloat16 [48, 48, 256, 256], P('energy', 'layer'), may hold values from -0.875 to 0.875
Outputs:
- lesser: bfloat16 [48, 48, 256, 256], P('energy', 'layer')
- self_energy: bfloat16 [48, 48, 256, 256], P('energy', 'layer')
The draws below stay inside these ranges and needn't reach their ends.
All inputs are finite; a program needn't handle non-finite values.
Results may differ from the reference program's by a relative error of at most 0.0095.
Values may be sent and summed in bfloat16 or wider, within the bound.
No kernel may reach another device: no remote copies, remote signals or barrier semaphores. Data moves between devices by JAX's collectives and lax.ppermute only.
A program may use at most 32 MiB of HBM per device.

```python
import jax
import jax.numpy as jnp
from jax import lax

ORB = 256
ITERS = 2
NE = 48
LAYERS = 48


def levels(own_key, shape, shards, low, top_value):
    loudness = 1.0
    for dim, shards_of in shards:
        heights = jax.random.uniform(jax.random.fold_in(jax.random.fold_in(own_key, 6), dim), (shards_of,), jnp.float32, low / len(shards), top_value / len(shards))
        loudness = loudness * jnp.repeat(jnp.exp(heights), shape[dim] // shards_of).reshape((-1,) + (1,) * (len(shape) - 1 - dim))
    return loudness


def gaussian(rng, shape, spread, limit, split=(), held_as=jnp.bfloat16):
    values = spread * jax.random.normal(rng, shape, jnp.float32)
    if split:
        values = values * levels(rng, shape, split, -0.22, 0.18)
    return jnp.clip(values, -limit, limit).astype(held_as)


def setup_inputs(seed: int = 0) -> dict:
    splits = jax.random.split(jax.random.key(seed), 4)
    return {
        "retarded": gaussian(splits[0], (NE, LAYERS, 3, ORB, ORB), ORB ** -0.5, 0.375, ((0, 48), (1, 16))),
        "scatter_in": gaussian(splits[1], (NE, LAYERS, ORB, ORB), 1.0, 6.0, ((0, 48), (1, 16))),
        "screen": gaussian(splits[2], (NE, LAYERS, ORB, ORB), NE ** -0.5, 0.875, ((0, 48), (1, 16))),
    }


def symmetric(matrix):
    matrix = matrix.astype(jnp.float32)
    return 0.5 * (matrix + jnp.swapaxes(matrix, -1, -2))


def lesser_energy(inputs_pair):
    retarded, coupling = inputs_pair
    layers = coupling.shape[0]
    padded = jnp.pad(coupling, ((1, 1), (0, 0), (0, 0)))
    running = jnp.zeros(coupling.shape, jnp.float32)
    for offset in range(3):
        neighbour = padded[offset:offset + layers].astype(jnp.float32)
        factor = retarded[:, offset].astype(jnp.float32)
        left_part = jnp.einsum("lab,lbc->lac", factor, neighbour).astype(jnp.bfloat16).astype(jnp.float32)
        running = running + jnp.einsum("lac,lbc->lab", left_part, factor)
    return symmetric(running).astype(jnp.bfloat16)


def convolve(inputs_pair):
    lesser, screened = inputs_pair
    energies = lesser.shape[0]
    spectrum = jnp.fft.rfft(lesser.astype(jnp.float32), n=2 * energies, axis=0)
    spectrum = spectrum * jnp.fft.rfft(screened.astype(jnp.float32), n=2 * energies, axis=0)
    return jnp.fft.irfft(spectrum, n=2 * energies, axis=0)[:energies].astype(jnp.bfloat16)


def reference(retarded, scatter_in, screen):
    base_part = symmetric(scatter_in)
    screened = symmetric(screen).astype(jnp.bfloat16)
    screened_layers = jnp.swapaxes(screened, 0, 1)
    correction = jnp.zeros(base_part.shape, jnp.float32)
    lesser = None
    self_energy = None
    for iteration in range(ITERS):
        coupling = (base_part + correction).astype(jnp.bfloat16)
        lesser = lax.map(lesser_energy, (retarded, coupling))
        self_layers = lax.map(convolve, (jnp.swapaxes(lesser, 0, 1), screened_layers))
        self_energy = jnp.swapaxes(self_layers, 0, 1)
        correction = self_energy.astype(jnp.float32)
    return lesser, self_energy
```

```python
import functools

import jax
import jax.numpy as jnp
from jax import lax
from jax.experimental import pallas as pl
from jax.experimental.pallas import tpu as pltpu
from jax.sharding import PartitionSpec as P

ITERS = 2


def symmetric(matrix):
    matrix = matrix.astype(jnp.float32)
    return 0.5 * (matrix + jnp.swapaxes(matrix, -1, -2))


def halo(cells, axis):
    count = lax.axis_size(axis)
    ends = count - 1
    below = lax.ppermute(cells[-1:], axis, [(i, i + 1) for i in range(ends)])
    above = lax.ppermute(cells[:1], axis, [(i + 1, i) for i in range(ends)])
    return below, above


def lesser_blocks(retarded, coupling, below, above):
    layers = coupling.shape[0]
    neighbours = (
        jnp.concatenate([below, coupling[: layers - 1]], axis=0),
        coupling,
        jnp.concatenate([coupling[1:], above], axis=0),
    )
    running = None
    for offset in range(3):
        factor = retarded[:, offset]
        left_part = jnp.einsum(
            "lab,lbc->lac", factor, neighbours[offset], preferred_element_type=jnp.float32
        ).astype(jnp.bfloat16)
        term_part = jnp.einsum(
            "lac,lbc->lab", left_part, factor, preferred_element_type=jnp.float32
        )
        running = term_part if running is None else running + term_part
    return symmetric(running).astype(jnp.bfloat16)


def _conv_kernel(l_ref, s_ref, o_ref, lf, sf, *, l_idx, s_idx):
    energies = o_ref.shape[0]

    def read(ref, idx, e):
        return ref[e] if idx is None else ref[e, idx]

    for e in range(energies):
        lf[e] = read(l_ref, l_idx, e).astype(jnp.float32)
        sf[e] = read(s_ref, s_idx, e).astype(jnp.float32)
    for e in range(energies):
        acc = lf[e] * sf[0]
        for j in range(1, e + 1):
            acc = acc + lf[e - j] * sf[j]
        o_ref[e] = acc.astype(o_ref.dtype)


def energy_convolve(l_arr, l_idx, s_arr, s_idx):
    energies = l_arr.shape[0]
    block = l_arr.shape[-2:]
    elems = energies * block[0] * block[1]
    kernel = functools.partial(_conv_kernel, l_idx=l_idx, s_idx=s_idx)
    return pl.pallas_call(
        kernel,
        out_shape=jax.ShapeDtypeStruct((energies,) + block, jnp.bfloat16),
        scratch_shapes=[
            pltpu.VMEM((energies,) + block, jnp.float32),
            pltpu.VMEM((energies,) + block, jnp.float32),
        ],
        cost_estimate=pl.CostEstimate(
            flops=elems * (energies + 1), bytes_accessed=elems * 6, transcendentals=0
        ),
    )(l_arr, s_arr)


def shards(retarded, scatter_in, screen):
    energies = lax.axis_size("energy")
    layers = retarded.shape[1]
    orbitals = retarded.shape[-1]
    rows = layers * orbitals // energies
    retarded = retarded[0]
    base_part = symmetric(scatter_in[0])
    screened = symmetric(screen[0]).astype(jnp.bfloat16)

    def to_columns(blocks):
        return blocks.reshape(energies, rows, orbitals)

    def to_blocks(columns):
        return columns.reshape(1, layers, orbitals, orbitals)

    correction = None
    screen_columns = None
    lesser = None
    self_energy = None
    for iteration in range(ITERS):
        if correction is None:
            coupling = base_part.astype(jnp.bfloat16)
        else:
            coupling = (base_part + correction).astype(jnp.bfloat16)
        below, above = halo(coupling, "layer")
        lesser = lesser_blocks(retarded, coupling, below, above)
        if screen_columns is None:
            both = jnp.stack([to_columns(lesser), to_columns(screened)], axis=1)
            screen_columns = lax.all_to_all(both, "energy", 0, 0, tiled=True)
            self_columns = energy_convolve(screen_columns, 0, screen_columns, 1)
        else:
            lesser_columns = lax.all_to_all(to_columns(lesser), "energy", 0, 0, tiled=True)
            self_columns = energy_convolve(lesser_columns, None, screen_columns, 1)
        returned = lax.all_to_all(self_columns, "energy", 0, 0, tiled=True)
        self_energy = to_blocks(returned)
        correction = self_energy[0].astype(jnp.float32)
    return (lesser[None], self_energy)


def solution(mesh):
    placed = (
        P("energy", "layer", None, None, None),
        P("energy", "layer", None, None),
        P("energy", "layer", None, None),
    )
    return jax.shard_map(
        shards,
        mesh=mesh,
        in_specs=placed,
        out_specs=(P("energy", "layer", None, None), P("energy", "layer", None, None)),
        check_vma=False,
    )
```

```python
import functools

import jax
import jax.numpy as jnp
from jax import lax
from jax.experimental import pallas as pl
from jax.experimental.pallas import tpu as pltpu
from jax.sharding import PartitionSpec as P

ITERS = 2


def symmetric(matrix):
    matrix = matrix.astype(jnp.float32)
    return 0.5 * (matrix + jnp.swapaxes(matrix, -1, -2))


def halo(cells, axis):
    count = lax.axis_size(axis)
    ends = count - 1
    below = lax.ppermute(cells[-1:], axis, [(i, i + 1) for i in range(ends)])
    above = lax.ppermute(cells[:1], axis, [(i + 1, i) for i in range(ends)])
    return below, above


def lesser_blocks(retarded, coupling, below, above):
    layers = coupling.shape[0]
    neighbours = (
        jnp.concatenate([below, coupling[: layers - 1]], axis=0),
        coupling,
        jnp.concatenate([coupling[1:], above], axis=0),
    )
    running = None
    for offset in range(3):
        factor = retarded[:, offset]
        left_part = jnp.einsum(
            "lab,lbc->lac", factor, neighbours[offset], preferred_element_type=jnp.float32
        ).astype(jnp.bfloat16)
        term_part = jnp.einsum(
            "lac,lbc->lab", left_part, factor, preferred_element_type=jnp.float32
        )
        running = term_part if running is None else running + term_part
    return symmetric(running).astype(jnp.bfloat16)


def _conv_kernel(l_ref, s_ref, o_ref, lf, sf, *, l_idx, s_idx):
    energies = o_ref.shape[0]

    def read(ref, idx, e):
        return ref[e] if idx is None else ref[e, idx]

    for e in range(energies):
        lf[e] = read(l_ref, l_idx, e).astype(jnp.float32)
        sf[e] = read(s_ref, s_idx, e).astype(jnp.float32)
    for e in range(energies):
        acc = lf[e] * sf[0]
        for j in range(1, e + 1):
            acc = acc + lf[e - j] * sf[j]
        o_ref[e] = acc.astype(o_ref.dtype)


def energy_convolve(l_arr, l_idx, s_arr, s_idx):
    energies = l_arr.shape[0]
    block = l_arr.shape[-2:]
    elems = energies * block[0] * block[1]
    kernel = functools.partial(_conv_kernel, l_idx=l_idx, s_idx=s_idx)
    return pl.pallas_call(
        kernel,
        out_shape=jax.ShapeDtypeStruct((energies,) + block, jnp.bfloat16),
        scratch_shapes=[
            pltpu.VMEM((energies,) + block, jnp.float32),
            pltpu.VMEM((energies,) + block, jnp.float32),
        ],
        cost_estimate=pl.CostEstimate(
            flops=elems * (energies + 1), bytes_accessed=elems * 6, transcendentals=0
        ),
    )(l_arr, s_arr)


def pack_symmetric(blocks):
    half = blocks.shape[-1] // 2
    rows = lax.broadcasted_iota(jnp.int32, (half, half), 0)
    cols = lax.broadcasted_iota(jnp.int32, (half, half), 1)
    top_left = blocks[:, :half, :half]
    bottom_right = blocks[:, half:, half:]
    folded = jnp.where(rows <= cols, top_left, bottom_right)
    diagonal = jnp.where(rows == cols, bottom_right, jnp.zeros_like(bottom_right))
    return jnp.concatenate([folded, blocks[:, :half, half:], diagonal], axis=-1)


def unpack_symmetric(packed):
    half = packed.shape[-1] // 3
    rows = lax.broadcasted_iota(jnp.int32, (half, half), 0)
    cols = lax.broadcasted_iota(jnp.int32, (half, half), 1)
    folded = packed[..., :half]
    off = packed[..., half : 2 * half]
    diagonal = packed[..., 2 * half :]
    flipped = jnp.swapaxes(folded, -1, -2)
    top_left = jnp.where(rows <= cols, folded, flipped)
    bottom_right = jnp.where(rows > cols, folded, flipped)
    bottom_right = jnp.where(rows == cols, diagonal, bottom_right)
    top = jnp.concatenate([top_left, off], axis=-1)
    bottom = jnp.concatenate([jnp.swapaxes(off, -1, -2), bottom_right], axis=-1)
    return jnp.concatenate([top, bottom], axis=-2)


def shards(retarded, scatter_in, screen):
    energies = lax.axis_size("energy")
    layers = retarded.shape[1]
    orbitals = retarded.shape[-1]
    half = orbitals // 2
    rows = layers * half // energies
    retarded = retarded[0]
    base_part = symmetric(scatter_in[0])
    screened = symmetric(screen[0]).astype(jnp.bfloat16)

    def to_columns(blocks):
        packed = pack_symmetric(blocks)
        return packed.reshape(energies, rows, packed.shape[-1])

    def to_blocks(columns):
        return unpack_symmetric(columns.reshape(layers, half, columns.shape[-1]))

    correction = None
    screen_columns = None
    lesser = None
    self_energy = None
    for iteration in range(ITERS):
        if correction is None:
            coupling = base_part.astype(jnp.bfloat16)
        else:
            coupling = (base_part + correction).astype(jnp.bfloat16)
        below, above = halo(coupling, "layer")
        lesser = lesser_blocks(retarded, coupling, below, above)
        if screen_columns is None:
            both = jnp.stack([to_columns(lesser), to_columns(screened)], axis=1)
            screen_columns = lax.all_to_all(both, "energy", 0, 0, tiled=True)
            self_columns = energy_convolve(screen_columns, 0, screen_columns, 1)
        else:
            lesser_columns = lax.all_to_all(to_columns(lesser), "energy", 0, 0, tiled=True)
            self_columns = energy_convolve(lesser_columns, None, screen_columns, 1)
        returned = lax.all_to_all(self_columns, "energy", 0, 0, tiled=True)
        self_blocks = to_blocks(returned)
        self_energy = self_blocks[None]
        correction = self_blocks.astype(jnp.float32)
    return (lesser[None], self_energy)


def solution(mesh):
    placed = (
        P("energy", "layer", None, None, None),
        P("energy", "layer", None, None),
        P("energy", "layer", None, None),
    )
    return jax.shard_map(
        shards,
        mesh=mesh,
        in_specs=placed,
        out_specs=(P("energy", "layer", None, None), P("energy", "layer", None, None)),
        check_vma=False,
    )
```

```python
import functools

import jax
import jax.numpy as jnp
from jax import lax
from jax.experimental import pallas as pl
from jax.experimental.pallas import tpu as pltpu
from jax.sharding import PartitionSpec as P

ITERS = 2


def symmetric(matrix):
    matrix = matrix.astype(jnp.float32)
    return 0.5 * (matrix + jnp.swapaxes(matrix, -1, -2))


def halo(cells, axis):
    count = lax.axis_size(axis)
    ends = count - 1
    below = lax.ppermute(cells[-1:], axis, [(i, i + 1) for i in range(ends)])
    above = lax.ppermute(cells[:1], axis, [(i + 1, i) for i in range(ends)])
    return below, above


def _lesser_kernel(r_ref, c_ref, below_ref, above_ref, o_ref):
    layers = c_ref.shape[0]

    def neighbour(index):
        if index < 0:
            return below_ref[0]
        if index >= layers:
            return above_ref[0]
        return c_ref[index]

    for layer in range(layers):
        running = None
        for offset in range(3):
            factor = r_ref[layer, offset]
            left_part = jnp.dot(
                factor, neighbour(layer + offset - 1), preferred_element_type=jnp.float32
            ).astype(jnp.bfloat16)
            term_part = lax.dot_general(
                left_part,
                factor,
                (((1,), (1,)), ((), ())),
                preferred_element_type=jnp.float32,
            )
            running = term_part if running is None else running + term_part
        o_ref[layer] = (0.5 * (running + running.T)).astype(o_ref.dtype)


def lesser_blocks(retarded, coupling, below, above):
    layers, n = coupling.shape[0], coupling.shape[-1]
    return pl.pallas_call(
        _lesser_kernel,
        out_shape=jax.ShapeDtypeStruct(coupling.shape, jnp.bfloat16),
        cost_estimate=pl.CostEstimate(
            flops=layers * 3 * 4 * n * n * n,
            bytes_accessed=(layers * 3 + layers + 2 + layers) * n * n * 2,
            transcendentals=0,
        ),
    )(retarded, coupling, below, above)


def _conv_kernel(l_ref, s_ref, o_ref, lf, sf, *, l_idx, s_idx):
    energies = o_ref.shape[0]

    def read(ref, idx, e):
        return ref[e] if idx is None else ref[e, idx]

    for e in range(energies):
        lf[e] = read(l_ref, l_idx, e).astype(jnp.float32)
        sf[e] = read(s_ref, s_idx, e).astype(jnp.float32)
    for e in range(energies):
        acc = lf[e] * sf[0]
        for j in range(1, e + 1):
            acc = acc + lf[e - j] * sf[j]
        o_ref[e] = acc.astype(o_ref.dtype)


def energy_convolve(l_arr, l_idx, s_arr, s_idx):
    energies = l_arr.shape[0]
    block = l_arr.shape[-2:]
    elems = energies * block[0] * block[1]
    kernel = functools.partial(_conv_kernel, l_idx=l_idx, s_idx=s_idx)
    return pl.pallas_call(
        kernel,
        out_shape=jax.ShapeDtypeStruct((energies,) + block, jnp.bfloat16),
        scratch_shapes=[
            pltpu.VMEM((energies,) + block, jnp.float32),
            pltpu.VMEM((energies,) + block, jnp.float32),
        ],
        cost_estimate=pl.CostEstimate(
            flops=elems * (energies + 1), bytes_accessed=elems * 6, transcendentals=0
        ),
    )(l_arr, s_arr)


def pack_symmetric(blocks):
    half = blocks.shape[-1] // 2
    rows = lax.broadcasted_iota(jnp.int32, (half, half), 0)
    cols = lax.broadcasted_iota(jnp.int32, (half, half), 1)
    top_left = blocks[:, :half, :half]
    bottom_right = blocks[:, half:, half:]
    folded = jnp.where(rows <= cols, top_left, bottom_right)
    diagonal = jnp.where(rows == cols, bottom_right, jnp.zeros_like(bottom_right))
    return jnp.concatenate([folded, blocks[:, :half, half:], diagonal], axis=-1)


def unpack_symmetric(packed):
    half = packed.shape[-1] // 3
    rows = lax.broadcasted_iota(jnp.int32, (half, half), 0)
    cols = lax.broadcasted_iota(jnp.int32, (half, half), 1)
    folded = packed[..., :half]
    off = packed[..., half : 2 * half]
    diagonal = packed[..., 2 * half :]
    flipped = jnp.swapaxes(folded, -1, -2)
    top_left = jnp.where(rows <= cols, folded, flipped)
    bottom_right = jnp.where(rows > cols, folded, flipped)
    bottom_right = jnp.where(rows == cols, diagonal, bottom_right)
    top = jnp.concatenate([top_left, off], axis=-1)
    bottom = jnp.concatenate([jnp.swapaxes(off, -1, -2), bottom_right], axis=-1)
    return jnp.concatenate([top, bottom], axis=-2)


def shards(retarded, scatter_in, screen):
    energies = lax.axis_size("energy")
    layers = retarded.shape[1]
    orbitals = retarded.shape[-1]
    half = orbitals // 2
    rows = layers * half // energies
    retarded = retarded[0]
    base_part = symmetric(scatter_in[0])
    screened = symmetric(screen[0]).astype(jnp.bfloat16)

    def to_columns(blocks):
        packed = pack_symmetric(blocks)
        return packed.reshape(energies, rows, packed.shape[-1])

    def to_blocks(columns):
        return unpack_symmetric(columns.reshape(layers, half, columns.shape[-1]))

    correction = None
    screen_columns = None
    lesser = None
    self_energy = None
    for iteration in range(ITERS):
        if correction is None:
            coupling = base_part.astype(jnp.bfloat16)
        else:
            coupling = (base_part + correction).astype(jnp.bfloat16)
        below, above = halo(coupling, "layer")
        lesser = lesser_blocks(retarded, coupling, below, above)
        if screen_columns is None:
            both = jnp.stack([to_columns(lesser), to_columns(screened)], axis=1)
            screen_columns = lax.all_to_all(both, "energy", 0, 0, tiled=True)
            self_columns = energy_convolve(screen_columns, 0, screen_columns, 1)
        else:
            lesser_columns = lax.all_to_all(to_columns(lesser), "energy", 0, 0, tiled=True)
            self_columns = energy_convolve(lesser_columns, None, screen_columns, 1)
        returned = lax.all_to_all(self_columns, "energy", 0, 0, tiled=True)
        self_blocks = to_blocks(returned)
        self_energy = self_blocks[None]
        correction = self_blocks.astype(jnp.float32)
    return (lesser[None], self_energy)


def solution(mesh):
    placed = (
        P("energy", "layer", None, None, None),
        P("energy", "layer", None, None),
        P("energy", "layer", None, None),
    )
    return jax.shard_map(
        shards,
        mesh=mesh,
        in_specs=placed,
        out_specs=(P("energy", "layer", None, None), P("energy", "layer", None, None)),
        check_vma=False,
    )
```

```python
import functools

import jax
import jax.numpy as jnp
from jax import lax
from jax.experimental import pallas as pl
from jax.experimental.pallas import tpu as pltpu
from jax.sharding import PartitionSpec as P

ITERS = 2


def symmetric(matrix):
    matrix = matrix.astype(jnp.float32)
    return 0.5 * (matrix + jnp.swapaxes(matrix, -1, -2))


def halo(cells, axis):
    count = lax.axis_size(axis)
    ends = count - 1
    below = lax.ppermute(cells[-1:], axis, [(i, i + 1) for i in range(ends)])
    above = lax.ppermute(cells[:1], axis, [(i + 1, i) for i in range(ends)])
    return below, above


def _lesser_kernel(r_ref, c_ref, below_ref, above_ref, o_ref):
    layers = c_ref.shape[0]

    def neighbour(index):
        if index < 0:
            return below_ref[0]
        if index >= layers:
            return above_ref[0]
        return c_ref[index]

    for layer in range(layers):
        running = None
        for offset in range(3):
            factor = r_ref[layer, offset]
            left_part = jnp.dot(
                factor, neighbour(layer + offset - 1), preferred_element_type=jnp.float32
            ).astype(jnp.bfloat16)
            term_part = lax.dot_general(
                left_part,
                factor,
                (((1,), (1,)), ((), ())),
                preferred_element_type=jnp.float32,
            )
            running = term_part if running is None else running + term_part
        o_ref[layer] = (0.5 * (running + running.T)).astype(o_ref.dtype)


def lesser_blocks(retarded, coupling, below, above):
    layers, n = coupling.shape[0], coupling.shape[-1]
    return pl.pallas_call(
        _lesser_kernel,
        out_shape=jax.ShapeDtypeStruct(coupling.shape, jnp.bfloat16),
        cost_estimate=pl.CostEstimate(
            flops=layers * 3 * 4 * n * n * n,
            bytes_accessed=(layers * 3 + layers + 2 + layers) * n * n * 2,
            transcendentals=0,
        ),
    )(retarded, coupling, below, above)


def _conv_core(lf, sf, o_ref):
    energies = o_ref.shape[0]
    for e in range(energies):
        acc = lf[e] * sf[0]
        for j in range(1, e + 1):
            acc = acc + lf[e - j] * sf[j]
        o_ref[e] = acc.astype(o_ref.dtype)


def _conv_first_kernel(x_ref, o_ref, s_out_ref, lf, sf):
    energies = o_ref.shape[0]
    h = x_ref.shape[-1] // 5
    for e in range(energies):
        lf[e, :, : 2 * h] = x_ref[e, :, : 2 * h].astype(jnp.float32)
        sf[e, :, : 2 * h] = x_ref[e, :, 2 * h : 4 * h].astype(jnp.float32)
        shared = x_ref[e, :, 4 * h :].astype(jnp.float32)
        lf[e, :, 2 * h :] = shared
        sf[e, :, 2 * h :] = pltpu.roll(shared, h // 2, 1)
    _conv_core(lf, sf, o_ref)
    s_out_ref[...] = sf[...].astype(s_out_ref.dtype)


def _conv_kernel(l_ref, s_ref, o_ref, lf, sf):
    energies = o_ref.shape[0]
    for e in range(energies):
        lf[e] = l_ref[e].astype(jnp.float32)
        sf[e] = s_ref[e].astype(jnp.float32)
    _conv_core(lf, sf, o_ref)


def _conv_call(kernel, outs, block, args):
    energies = block[0]
    elems = block[0] * block[1] * block[2]
    return pl.pallas_call(
        kernel,
        out_shape=outs,
        scratch_shapes=[pltpu.VMEM(block, jnp.float32), pltpu.VMEM(block, jnp.float32)],
        cost_estimate=pl.CostEstimate(
            flops=elems * (energies + 1), bytes_accessed=elems * 8, transcendentals=0
        ),
    )(*args)


def energy_convolve_first(x):
    energies, rows, width = x.shape
    block = (energies, rows, width // 5 * 3)
    outs = (jax.ShapeDtypeStruct(block, jnp.bfloat16), jax.ShapeDtypeStruct(block, jnp.bfloat16))
    return _conv_call(_conv_first_kernel, outs, block, (x,))


def energy_convolve(l_arr, s_arr):
    block = l_arr.shape
    return _conv_call(_conv_kernel, jax.ShapeDtypeStruct(block, jnp.bfloat16), block, (l_arr, s_arr))


def pack_symmetric(blocks):
    half = blocks.shape[-1] // 2
    rows = lax.broadcasted_iota(jnp.int32, (half, half), 0)
    cols = lax.broadcasted_iota(jnp.int32, (half, half), 1)
    top_left = blocks[:, :half, :half]
    bottom_right = blocks[:, half:, half:]
    folded = jnp.where(rows <= cols, top_left, bottom_right)
    diagonal = jnp.where(rows == cols, bottom_right, jnp.zeros_like(bottom_right))
    return jnp.concatenate([folded, blocks[:, :half, half:], diagonal], axis=-1)


def pack_symmetric_pair(first, second):
    half = first.shape[-1] // 2
    rows = lax.broadcasted_iota(jnp.int32, (half, half), 0)
    cols = lax.broadcasted_iota(jnp.int32, (half, half), 1)
    a = pack_symmetric(first)
    b = pack_symmetric(second)
    moved = jnp.roll(b[..., 2 * half :], half // 2, axis=-1)
    shared = jnp.where(rows == cols, a[..., 2 * half :], moved)
    return jnp.concatenate([a[..., : 2 * half], b[..., : 2 * half], shared], axis=-1)


def unpack_symmetric(packed):
    half = packed.shape[-1] // 3
    rows = lax.broadcasted_iota(jnp.int32, (half, half), 0)
    cols = lax.broadcasted_iota(jnp.int32, (half, half), 1)
    folded = packed[..., :half]
    off = packed[..., half : 2 * half]
    diagonal = packed[..., 2 * half :]
    flipped = jnp.swapaxes(folded, -1, -2)
    top_left = jnp.where(rows <= cols, folded, flipped)
    bottom_right = jnp.where(rows > cols, folded, flipped)
    bottom_right = jnp.where(rows == cols, diagonal, bottom_right)
    top = jnp.concatenate([top_left, off], axis=-1)
    bottom = jnp.concatenate([jnp.swapaxes(off, -1, -2), bottom_right], axis=-1)
    return jnp.concatenate([top, bottom], axis=-2)


def shards(retarded, scatter_in, screen):
    energies = lax.axis_size("energy")
    layers = retarded.shape[1]
    orbitals = retarded.shape[-1]
    half = orbitals // 2
    rows = layers * half // energies
    retarded = retarded[0]
    base_part = symmetric(scatter_in[0])
    screened = symmetric(screen[0]).astype(jnp.bfloat16)

    def to_columns(blocks):
        packed = pack_symmetric(blocks)
        return packed.reshape(energies, rows, packed.shape[-1])

    def to_blocks(columns):
        return unpack_symmetric(columns.reshape(layers, half, columns.shape[-1]))

    correction = None
    screen_columns = None
    lesser = None
    self_energy = None
    for iteration in range(ITERS):
        if correction is None:
            coupling = base_part.astype(jnp.bfloat16)
        else:
            coupling = (base_part + correction).astype(jnp.bfloat16)
        below, above = halo(coupling, "layer")
        lesser = lesser_blocks(retarded, coupling, below, above)
        if screen_columns is None:
            both = pack_symmetric_pair(lesser, screened)
            both = lax.all_to_all(
                both.reshape(energies, rows, both.shape[-1]), "energy", 0, 0, tiled=True
            )
            self_columns, screen_columns = energy_convolve_first(both)
        else:
            lesser_columns = lax.all_to_all(to_columns(lesser), "energy", 0, 0, tiled=True)
            self_columns = energy_convolve(lesser_columns, screen_columns)
        returned = lax.all_to_all(self_columns, "energy", 0, 0, tiled=True)
        self_blocks = to_blocks(returned)
        self_energy = self_blocks[None]
        correction = self_blocks.astype(jnp.float32)
    return (lesser[None], self_energy)


def solution(mesh):
    placed = (
        P("energy", "layer", None, None, None),
        P("energy", "layer", None, None),
        P("energy", "layer", None, None),
    )
    return jax.shard_map(
        shards,
        mesh=mesh,
        in_specs=placed,
        out_specs=(P("energy", "layer", None, None), P("energy", "layer", None, None)),
        check_vma=False,
    )
```

```python
import functools

import jax
import jax.numpy as jnp
from jax import lax
from jax.experimental import pallas as pl
from jax.experimental.pallas import tpu as pltpu
from jax.sharding import PartitionSpec as P

ITERS = 2


def symmetric(matrix):
    matrix = matrix.astype(jnp.float32)
    return 0.5 * (matrix + jnp.swapaxes(matrix, -1, -2))


def halo(cells, axis):
    count = lax.axis_size(axis)
    ends = count - 1
    below = lax.ppermute(cells[-1:], axis, [(i, i + 1) for i in range(ends)])
    above = lax.ppermute(cells[:1], axis, [(i + 1, i) for i in range(ends)])
    return below, above


def _lesser_kernel(r_ref, c_ref, below_ref, above_ref, o_ref):
    layers = c_ref.shape[0]

    def neighbour(index):
        if index < 0:
            return below_ref[0]
        if index >= layers:
            return above_ref[0]
        return c_ref[index]

    for layer in range(layers):
        running = None
        for offset in range(3):
            factor = r_ref[layer, offset]
            left_part = jnp.dot(
                factor, neighbour(layer + offset - 1), preferred_element_type=jnp.float32
            ).astype(jnp.bfloat16)
            term_part = lax.dot_general(
                left_part,
                factor,
                (((1,), (1,)), ((), ())),
                preferred_element_type=jnp.float32,
            )
            running = term_part if running is None else running + term_part
        o_ref[layer] = (0.5 * (running + running.T)).astype(o_ref.dtype)


def lesser_blocks(retarded, coupling, below, above):
    layers, n = coupling.shape[0], coupling.shape[-1]
    return pl.pallas_call(
        _lesser_kernel,
        out_shape=jax.ShapeDtypeStruct(coupling.shape, jnp.bfloat16),
        cost_estimate=pl.CostEstimate(
            flops=layers * 3 * 4 * n * n * n,
            bytes_accessed=(layers * 3 + layers + 2 + layers) * n * n * 2,
            transcendentals=0,
        ),
    )(retarded, coupling, below, above)


def _conv_core(lf, sf, o_ref, group=4):
    energies = o_ref.shape[0]
    for first in range(0, energies, group):
        last = min(first + group, energies)
        acc = [None] * (last - first)
        window = {}
        for j in range(last):
            s_row = sf[j]
            for e in range(max(first, j), last):
                if e - j not in window:
                    window[e - j] = lf[e - j]
                term = window[e - j] * s_row
                k = e - first
                acc[k] = term if acc[k] is None else acc[k] + term
            window.pop(last - 1 - j, None)
        for k in range(last - first):
            o_ref[first + k] = acc[k].astype(o_ref.dtype)


def _conv_first_kernel(x_ref, o_ref, s_out_ref, lf, sf):
    energies = o_ref.shape[0]
    h = x_ref.shape[-1] // 5
    for e in range(energies):
        lf[e, :, : 2 * h] = x_ref[e, :, : 2 * h].astype(jnp.float32)
        sf[e, :, : 2 * h] = x_ref[e, :, 2 * h : 4 * h].astype(jnp.float32)
        shared = x_ref[e, :, 4 * h :].astype(jnp.float32)
        lf[e, :, 2 * h :] = shared
        sf[e, :, 2 * h :] = pltpu.roll(shared, h // 2, 1)
    _conv_core(lf, sf, o_ref)
    s_out_ref[...] = sf[...].astype(s_out_ref.dtype)


def _conv_kernel(l_ref, s_ref, o_ref, lf, sf):
    energies = o_ref.shape[0]
    for e in range(energies):
        lf[e] = l_ref[e].astype(jnp.float32)
        sf[e] = s_ref[e].astype(jnp.float32)
    _conv_core(lf, sf, o_ref)


def _conv_call(kernel, outs, block, args):
    energies = block[0]
    elems = block[0] * block[1] * block[2]
    return pl.pallas_call(
        kernel,
        out_shape=outs,
        scratch_shapes=[pltpu.VMEM(block, jnp.float32), pltpu.VMEM(block, jnp.float32)],
        cost_estimate=pl.CostEstimate(
            flops=elems * (energies + 1), bytes_accessed=elems * 8, transcendentals=0
        ),
    )(*args)


def energy_convolve_first(x):
    energies, rows, width = x.shape
    block = (energies, rows, width // 5 * 3)
    outs = (jax.ShapeDtypeStruct(block, jnp.bfloat16), jax.ShapeDtypeStruct(block, jnp.bfloat16))
    return _conv_call(_conv_first_kernel, outs, block, (x,))


def energy_convolve(l_arr, s_arr):
    block = l_arr.shape
    return _conv_call(_conv_kernel, jax.ShapeDtypeStruct(block, jnp.bfloat16), block, (l_arr, s_arr))


def pack_symmetric(blocks):
    half = blocks.shape[-1] // 2
    rows = lax.broadcasted_iota(jnp.int32, (half, half), 0)
    cols = lax.broadcasted_iota(jnp.int32, (half, half), 1)
    top_left = blocks[:, :half, :half]
    bottom_right = blocks[:, half:, half:]
    folded = jnp.where(rows <= cols, top_left, bottom_right)
    diagonal = jnp.where(rows == cols, bottom_right, jnp.zeros_like(bottom_right))
    return jnp.concatenate([folded, blocks[:, :half, half:], diagonal], axis=-1)


def pack_symmetric_pair(first, second):
    half = first.shape[-1] // 2
    rows = lax.broadcasted_iota(jnp.int32, (half, half), 0)
    cols = lax.broadcasted_iota(jnp.int32, (half, half), 1)
    a = pack_symmetric(first)
    b = pack_symmetric(second)
    moved = jnp.roll(b[..., 2 * half :], half // 2, axis=-1)
    shared = jnp.where(rows == cols, a[..., 2 * half :], moved)
    return jnp.concatenate([a[..., : 2 * half], b[..., : 2 * half], shared], axis=-1)


def unpack_symmetric(packed):
    half = packed.shape[-1] // 3
    rows = lax.broadcasted_iota(jnp.int32, (half, half), 0)
    cols = lax.broadcasted_iota(jnp.int32, (half, half), 1)
    folded = packed[..., :half]
    off = packed[..., half : 2 * half]
    diagonal = packed[..., 2 * half :]
    flipped = jnp.swapaxes(folded, -1, -2)
    top_left = jnp.where(rows <= cols, folded, flipped)
    bottom_right = jnp.where(rows > cols, folded, flipped)
    bottom_right = jnp.where(rows == cols, diagonal, bottom_right)
    top = jnp.concatenate([top_left, off], axis=-1)
    bottom = jnp.concatenate([jnp.swapaxes(off, -1, -2), bottom_right], axis=-1)
    return jnp.concatenate([top, bottom], axis=-2)


def shards(retarded, scatter_in, screen):
    energies = lax.axis_size("energy")
    layers = retarded.shape[1]
    orbitals = retarded.shape[-1]
    half = orbitals // 2
    rows = layers * half // energies
    retarded = retarded[0]
    base_part = symmetric(scatter_in[0])
    screened = symmetric(screen[0]).astype(jnp.bfloat16)

    def to_columns(blocks):
        packed = pack_symmetric(blocks)
        return packed.reshape(energies, rows, packed.shape[-1])

    def to_blocks(columns):
        return unpack_symmetric(columns.reshape(layers, half, columns.shape[-1]))

    correction = None
    screen_columns = None
    lesser = None
    self_energy = None
    for iteration in range(ITERS):
        if correction is None:
            coupling = base_part.astype(jnp.bfloat16)
        else:
            coupling = (base_part + correction).astype(jnp.bfloat16)
        below, above = halo(coupling, "layer")
        lesser = lesser_blocks(retarded, coupling, below, above)
        if screen_columns is None:
            both = pack_symmetric_pair(lesser, screened)
            both = lax.all_to_all(
                both.reshape(energies, rows, both.shape[-1]), "energy", 0, 0, tiled=True
            )
            self_columns, screen_columns = energy_convolve_first(both)
        else:
            lesser_columns = lax.all_to_all(to_columns(lesser), "energy", 0, 0, tiled=True)
            self_columns = energy_convolve(lesser_columns, screen_columns)
        returned = lax.all_to_all(self_columns, "energy", 0, 0, tiled=True)
        self_blocks = to_blocks(returned)
        self_energy = self_blocks[None]
        correction = self_blocks.astype(jnp.float32)
    return (lesser[None], self_energy)


def solution(mesh):
    placed = (
        P("energy", "layer", None, None, None),
        P("energy", "layer", None, None),
        P("energy", "layer", None, None),
    )
    return jax.shard_map(
        shards,
        mesh=mesh,
        in_specs=placed,
        out_specs=(P("energy", "layer", None, None), P("energy", "layer", None, None)),
        check_vma=False,
    )
```

```python
import functools

import jax
import jax.numpy as jnp
from jax import lax
from jax.experimental import pallas as pl
from jax.experimental.pallas import tpu as pltpu
from jax.sharding import PartitionSpec as P

ITERS = 2


def symmetric(matrix):
    matrix = matrix.astype(jnp.float32)
    return 0.5 * (matrix + jnp.swapaxes(matrix, -1, -2))


def halo(cells, axis):
    count = lax.axis_size(axis)
    ends = count - 1
    below = lax.ppermute(cells[-1:], axis, [(i, i + 1) for i in range(ends)])
    above = lax.ppermute(cells[:1], axis, [(i + 1, i) for i in range(ends)])
    return below, above


def _lesser_kernel(r_ref, c_ref, below_ref, above_ref, *rest):
    if len(rest) == 3:
        screen_ref, o_ref, packed_ref = rest
    else:
        screen_ref, (o_ref, packed_ref) = None, rest
    layers = c_ref.shape[0]
    n = c_ref.shape[-1]
    h = n // 2
    rows = lax.broadcasted_iota(jnp.int32, (h, h), 0)
    cols = lax.broadcasted_iota(jnp.int32, (h, h), 1)

    def neighbour(index):
        if index < 0:
            return below_ref[0]
        if index >= layers:
            return above_ref[0]
        return c_ref[index]

    for layer in range(layers):
        running = None
        for offset in range(3):
            factor = r_ref[layer, offset]
            left_part = jnp.dot(
                factor, neighbour(layer + offset - 1), preferred_element_type=jnp.float32
            ).astype(jnp.bfloat16)
            term_part = lax.dot_general(
                left_part,
                factor,
                (((1,), (1,)), ((), ())),
                preferred_element_type=jnp.float32,
            )
            running = term_part if running is None else running + term_part
        block = (0.5 * (running + running.T)).astype(o_ref.dtype)
        o_ref[layer] = block
        top_left = block[:h, :h]
        bottom_right = block[h:, h:]
        packed_ref[layer, :, :h] = jnp.where(rows <= cols, top_left, bottom_right)
        packed_ref[layer, :, h : 2 * h] = block[:h, h:]
        if screen_ref is None:
            packed_ref[layer, :, 2 * h :] = jnp.where(
                rows == cols, bottom_right, jnp.zeros_like(bottom_right)
            )
        else:
            packed_ref[layer, :, 2 * h : 4 * h] = screen_ref[layer, :, : 2 * h]
            packed_ref[layer, :, 4 * h :] = jnp.where(
                rows == cols, bottom_right, screen_ref[layer, :, 2 * h :]
            )


def lesser_blocks(retarded, coupling, below, above, screen_packed=None):
    layers, n = coupling.shape[0], coupling.shape[-1]
    width = 3 * n // 2 if screen_packed is None else 5 * n // 2
    args = (retarded, coupling, below, above)
    if screen_packed is not None:
        args = args + (screen_packed,)
    return pl.pallas_call(
        _lesser_kernel,
        out_shape=(
            jax.ShapeDtypeStruct(coupling.shape, jnp.bfloat16),
            jax.ShapeDtypeStruct((layers, n // 2, width), jnp.bfloat16),
        ),
        cost_estimate=pl.CostEstimate(
            flops=layers * 3 * 4 * n * n * n,
            bytes_accessed=(layers * 3 + layers + 2 + layers * 2) * n * n * 2,
            transcendentals=0,
        ),
    )(*args)


def _conv_core(lf, sf, o_ref, group=4):
    energies = o_ref.shape[0]
    for first in range(0, energies, group):
        last = min(first + group, energies)
        acc = [None] * (last - first)
        window = {}
        for j in range(last):
            s_row = sf[j]
            for e in range(max(first, j), last):
                if e - j not in window:
                    window[e - j] = lf[e - j]
                term = window[e - j] * s_row
                k = e - first
                acc[k] = term if acc[k] is None else acc[k] + term
            window.pop(last - 1 - j, None)
        for k in range(last - first):
            o_ref[first + k] = acc[k].astype(o_ref.dtype)


def _conv_first_kernel(x_ref, o_ref, s_out_ref, lf, sf):
    energies = o_ref.shape[0]
    h = x_ref.shape[-1] // 5
    for e in range(energies):
        lf[e, :, : 2 * h] = x_ref[e, :, : 2 * h].astype(jnp.float32)
        sf[e, :, : 2 * h] = x_ref[e, :, 2 * h : 4 * h].astype(jnp.float32)
        shared = x_ref[e, :, 4 * h :].astype(jnp.float32)
        lf[e, :, 2 * h :] = shared
        sf[e, :, 2 * h :] = pltpu.roll(shared, h // 2, 1)
    _conv_core(lf, sf, o_ref)
    s_out_ref[...] = sf[...].astype(s_out_ref.dtype)


def _conv_kernel(l_ref, s_ref, o_ref, lf, sf):
    energies = o_ref.shape[0]
    for e in range(energies):
        lf[e] = l_ref[e].astype(jnp.float32)
        sf[e] = s_ref[e].astype(jnp.float32)
    _conv_core(lf, sf, o_ref)


def _conv_call(kernel, outs, block, args):
    energies = block[0]
    elems = block[0] * block[1] * block[2]
    return pl.pallas_call(
        kernel,
        out_shape=outs,
        scratch_shapes=[pltpu.VMEM(block, jnp.float32), pltpu.VMEM(block, jnp.float32)],
        cost_estimate=pl.CostEstimate(
            flops=elems * (energies + 1), bytes_accessed=elems * 8, transcendentals=0
        ),
    )(*args)


def energy_convolve_first(x):
    energies, rows, width = x.shape
    block = (energies, rows, width // 5 * 3)
    outs = (jax.ShapeDtypeStruct(block, jnp.bfloat16), jax.ShapeDtypeStruct(block, jnp.bfloat16))
    return _conv_call(_conv_first_kernel, outs, block, (x,))


def energy_convolve(l_arr, s_arr):
    block = l_arr.shape
    return _conv_call(_conv_kernel, jax.ShapeDtypeStruct(block, jnp.bfloat16), block, (l_arr, s_arr))


def pack_symmetric(blocks):
    half = blocks.shape[-1] // 2
    rows = lax.broadcasted_iota(jnp.int32, (half, half), 0)
    cols = lax.broadcasted_iota(jnp.int32, (half, half), 1)
    top_left = blocks[:, :half, :half]
    bottom_right = blocks[:, half:, half:]
    folded = jnp.where(rows <= cols, top_left, bottom_right)
    diagonal = jnp.where(rows == cols, bottom_right, jnp.zeros_like(bottom_right))
    return jnp.concatenate([folded, blocks[:, :half, half:], diagonal], axis=-1)


def pack_screened(blocks):
    half = blocks.shape[-1] // 2
    packed = pack_symmetric(blocks)
    moved = jnp.roll(packed[..., 2 * half :], half // 2, axis=-1)
    return jnp.concatenate([packed[..., : 2 * half], moved], axis=-1)


def unpack_symmetric(packed):
    half = packed.shape[-1] // 3
    rows = lax.broadcasted_iota(jnp.int32, (half, half), 0)
    cols = lax.broadcasted_iota(jnp.int32, (half, half), 1)
    folded = packed[..., :half]
    off = packed[..., half : 2 * half]
    diagonal = packed[..., 2 * half :]
    flipped = jnp.swapaxes(folded, -1, -2)
    top_left = jnp.where(rows <= cols, folded, flipped)
    bottom_right = jnp.where(rows > cols, folded, flipped)
    bottom_right = jnp.where(rows == cols, diagonal, bottom_right)
    top = jnp.concatenate([top_left, off], axis=-1)
    bottom = jnp.concatenate([jnp.swapaxes(off, -1, -2), bottom_right], axis=-1)
    return jnp.concatenate([top, bottom], axis=-2)


def shards(retarded, scatter_in, screen):
    energies = lax.axis_size("energy")
    layers = retarded.shape[1]
    orbitals = retarded.shape[-1]
    half = orbitals // 2
    rows = layers * half // energies
    retarded = retarded[0]
    base_part = symmetric(scatter_in[0])
    screened = symmetric(screen[0]).astype(jnp.bfloat16)

    def to_blocks(columns):
        return unpack_symmetric(columns.reshape(layers, half, columns.shape[-1]))

    correction = None
    screen_columns = None
    lesser = None
    self_energy = None
    for iteration in range(ITERS):
        if correction is None:
            coupling = base_part.astype(jnp.bfloat16)
        else:
            coupling = (base_part + correction).astype(jnp.bfloat16)
        below, above = halo(coupling, "layer")
        if screen_columns is None:
            lesser, both = lesser_blocks(retarded, coupling, below, above, pack_screened(screened))
            both = lax.all_to_all(
                both.reshape(energies, rows, both.shape[-1]), "energy", 0, 0, tiled=True
            )
            self_columns, screen_columns = energy_convolve_first(both)
        else:
            lesser, packed = lesser_blocks(retarded, coupling, below, above)
            lesser_columns = lax.all_to_all(
                packed.reshape(energies, rows, packed.shape[-1]), "energy", 0, 0, tiled=True
            )
            self_columns = energy_convolve(lesser_columns, screen_columns)
        returned = lax.all_to_all(self_columns, "energy", 0, 0, tiled=True)
        self_blocks = to_blocks(returned)
        self_energy = self_blocks[None]
        correction = self_blocks.astype(jnp.float32)
    return (lesser[None], self_energy)


def solution(mesh):
    placed = (
        P("energy", "layer", None, None, None),
        P("energy", "layer", None, None),
        P("energy", "layer", None, None),
    )
    return jax.shard_map(
        shards,
        mesh=mesh,
        in_specs=placed,
        out_specs=(P("energy", "layer", None, None), P("energy", "layer", None, None)),
        check_vma=False,
    )
```

```python
import functools

import jax
import jax.numpy as jnp
from jax import lax
from jax.experimental import pallas as pl
from jax.experimental.pallas import tpu as pltpu
from jax.sharding import PartitionSpec as P

ITERS = 2


def symmetric(matrix):
    matrix = matrix.astype(jnp.float32)
    return 0.5 * (matrix + jnp.swapaxes(matrix, -1, -2))


def halo(cells, axis):
    count = lax.axis_size(axis)
    ends = count - 1
    below = lax.ppermute(cells[-1:], axis, [(i, i + 1) for i in range(ends)])
    above = lax.ppermute(cells[:1], axis, [(i + 1, i) for i in range(ends)])
    return below, above


def _lesser_kernel(r_ref, c_ref, below_ref, above_ref, *rest):
    if len(rest) == 3:
        screen_ref, o_ref, packed_ref = rest
    else:
        screen_ref, (o_ref, packed_ref) = None, rest
    layers = c_ref.shape[0]
    n = c_ref.shape[-1]
    h = n // 2
    rows = lax.broadcasted_iota(jnp.int32, (h, h), 0)
    cols = lax.broadcasted_iota(jnp.int32, (h, h), 1)

    def neighbour(index):
        if index < 0:
            return below_ref[0]
        if index >= layers:
            return above_ref[0]
        return c_ref[index]

    for layer in range(layers):
        running = None
        for offset in range(3):
            factor = r_ref[layer, offset]
            left_part = jnp.dot(
                factor, neighbour(layer + offset - 1), preferred_element_type=jnp.float32
            ).astype(jnp.bfloat16)
            term_part = lax.dot_general(
                left_part,
                factor,
                (((1,), (1,)), ((), ())),
                preferred_element_type=jnp.float32,
            )
            running = term_part if running is None else running + term_part
        block = (0.5 * (running + running.T)).astype(o_ref.dtype)
        o_ref[layer] = block
        top_left = block[:h, :h]
        bottom_right = block[h:, h:]
        packed_ref[layer, :, :h] = jnp.where(rows <= cols, top_left, bottom_right)
        packed_ref[layer, :, h : 2 * h] = block[:h, h:]
        if screen_ref is None:
            packed_ref[layer, :, 2 * h :] = jnp.where(
                rows == cols, bottom_right, jnp.zeros_like(bottom_right)
            )
        else:
            packed_ref[layer, :, 2 * h : 4 * h] = screen_ref[layer, :, : 2 * h]
            packed_ref[layer, :, 4 * h :] = jnp.where(
                rows == cols, bottom_right, screen_ref[layer, :, 2 * h :]
            )


def lesser_blocks(retarded, coupling, below, above, screen_packed=None):
    layers, n = coupling.shape[0], coupling.shape[-1]
    width = 3 * n // 2 if screen_packed is None else 5 * n // 2
    args = (retarded, coupling, below, above)
    if screen_packed is not None:
        args = args + (screen_packed,)
    return pl.pallas_call(
        _lesser_kernel,
        out_shape=(
            jax.ShapeDtypeStruct(coupling.shape, jnp.bfloat16),
            jax.ShapeDtypeStruct((layers, n // 2, width), jnp.bfloat16),
        ),
        cost_estimate=pl.CostEstimate(
            flops=layers * 3 * 4 * n * n * n,
            bytes_accessed=(layers * 3 + layers + 2 + layers * 2) * n * n * 2,
            transcendentals=0,
        ),
    )(*args)


def _conv_core(lf, sf, o_ref, group=4):
    energies = o_ref.shape[0]
    for first in range(0, energies, group):
        last = min(first + group, energies)
        acc = [None] * (last - first)
        window = {}
        for j in range(last):
            s_row = sf[j]
            for e in range(max(first, j), last):
                if e - j not in window:
                    window[e - j] = lf[e - j]
                term = window[e - j] * s_row
                k = e - first
                acc[k] = term if acc[k] is None else acc[k] + term
            window.pop(last - 1 - j, None)
        for k in range(last - first):
            o_ref[first + k] = acc[k].astype(o_ref.dtype)


def _conv_first_kernel(x_ref, o_ref, s_out_ref, lf, sf):
    energies = o_ref.shape[0]
    h = x_ref.shape[-1] // 5
    for e in range(energies):
        lf[e, :, : 2 * h] = x_ref[e, :, : 2 * h].astype(jnp.float32)
        sf[e, :, : 2 * h] = x_ref[e, :, 2 * h : 4 * h].astype(jnp.float32)
        shared = x_ref[e, :, 4 * h :].astype(jnp.float32)
        lf[e, :, 2 * h :] = shared
        sf[e, :, 2 * h :] = pltpu.roll(shared, h // 2, 1)
    _conv_core(lf, sf, o_ref)
    s_out_ref[...] = sf[...].astype(s_out_ref.dtype)


def _conv_kernel(l_ref, s_ref, o_ref, lf, sf):
    energies = o_ref.shape[0]
    for e in range(energies):
        lf[e] = l_ref[e].astype(jnp.float32)
        sf[e] = s_ref[e].astype(jnp.float32)
    _conv_core(lf, sf, o_ref)


def _conv_call(kernel, outs, block, args):
    energies = block[0]
    elems = block[0] * block[1] * block[2]
    return pl.pallas_call(
        kernel,
        out_shape=outs,
        scratch_shapes=[pltpu.VMEM(block, jnp.float32), pltpu.VMEM(block, jnp.float32)],
        cost_estimate=pl.CostEstimate(
            flops=elems * (energies + 1), bytes_accessed=elems * 8, transcendentals=0
        ),
    )(*args)


def energy_convolve_first(x):
    energies, rows, width = x.shape
    block = (energies, rows, width // 5 * 3)
    outs = (jax.ShapeDtypeStruct(block, jnp.bfloat16), jax.ShapeDtypeStruct(block, jnp.bfloat16))
    return _conv_call(_conv_first_kernel, outs, block, (x,))


def energy_convolve(l_arr, s_arr):
    block = l_arr.shape
    return _conv_call(_conv_kernel, jax.ShapeDtypeStruct(block, jnp.bfloat16), block, (l_arr, s_arr))


def pack_symmetric(blocks):
    half = blocks.shape[-1] // 2
    rows = lax.broadcasted_iota(jnp.int32, (half, half), 0)
    cols = lax.broadcasted_iota(jnp.int32, (half, half), 1)
    top_left = blocks[:, :half, :half]
    bottom_right = blocks[:, half:, half:]
    folded = jnp.where(rows <= cols, top_left, bottom_right)
    diagonal = jnp.where(rows == cols, bottom_right, jnp.zeros_like(bottom_right))
    return jnp.concatenate([folded, blocks[:, :half, half:], diagonal], axis=-1)


def pack_screened(blocks):
    half = blocks.shape[-1] // 2
    packed = pack_symmetric(blocks)
    moved = jnp.roll(packed[..., 2 * half :], half // 2, axis=-1)
    return jnp.concatenate([packed[..., : 2 * half], moved], axis=-1)


def unpack_symmetric(packed):
    half = packed.shape[-1] // 3
    rows = lax.broadcasted_iota(jnp.int32, (half, half), 0)
    cols = lax.broadcasted_iota(jnp.int32, (half, half), 1)
    folded = packed[..., :half]
    off = packed[..., half : 2 * half]
    diagonal = packed[..., 2 * half :]
    flipped = jnp.swapaxes(folded, -1, -2)
    top_left = jnp.where(rows <= cols, folded, flipped)
    bottom_right = jnp.where(rows > cols, folded, flipped)
    bottom_right = jnp.where(rows == cols, diagonal, bottom_right)
    top = jnp.concatenate([top_left, off], axis=-1)
    bottom = jnp.concatenate([jnp.swapaxes(off, -1, -2), bottom_right], axis=-1)
    return jnp.concatenate([top, bottom], axis=-2)


def shards(retarded, scatter_in, screen):
    energies = lax.axis_size("energy")
    layers = retarded.shape[1]
    orbitals = retarded.shape[-1]
    half = orbitals // 2
    rows = layers * half // energies
    retarded = retarded[0]
    base_part = symmetric(scatter_in[0])
    screened = symmetric(screen[0]).astype(jnp.bfloat16)

    def to_blocks(columns):
        return unpack_symmetric(columns.reshape(layers, half, columns.shape[-1]))

    correction = None
    screen_columns = None
    lesser = None
    self_energy = None
    for iteration in range(ITERS):
        if correction is None:
            coupling = base_part.astype(jnp.bfloat16)
        else:
            coupling = (base_part + correction).astype(jnp.bfloat16)
        if screen_columns is None:
            below, above = halo(scatter_in[0], "layer")
            below = symmetric(below).astype(jnp.bfloat16)
            above = symmetric(above).astype(jnp.bfloat16)
        else:
            below, above = halo(coupling, "layer")
        if screen_columns is None:
            lesser, both = lesser_blocks(retarded, coupling, below, above, pack_screened(screened))
            both = lax.all_to_all(
                both.reshape(energies, rows, both.shape[-1]), "energy", 0, 0, tiled=True
            )
            self_columns, screen_columns = energy_convolve_first(both)
        else:
            lesser, packed = lesser_blocks(retarded, coupling, below, above)
            lesser_columns = lax.all_to_all(
                packed.reshape(energies, rows, packed.shape[-1]), "energy", 0, 0, tiled=True
            )
            self_columns = energy_convolve(lesser_columns, screen_columns)
        returned = lax.all_to_all(self_columns, "energy", 0, 0, tiled=True)
        self_blocks = to_blocks(returned)
        self_energy = self_blocks[None]
        correction = self_blocks.astype(jnp.float32)
    return (lesser[None], self_energy)


def solution(mesh):
    placed = (
        P("energy", "layer", None, None, None),
        P("energy", "layer", None, None),
        P("energy", "layer", None, None),
    )
    return jax.shard_map(
        shards,
        mesh=mesh,
        in_specs=placed,
        out_specs=(P("energy", "layer", None, None), P("energy", "layer", None, None)),
        check_vma=False,
    )
```

```python
import functools

import jax
import jax.numpy as jnp
from jax import lax
from jax.experimental import pallas as pl
from jax.experimental.pallas import tpu as pltpu
from jax.sharding import PartitionSpec as P

ITERS = 2


def symmetric(matrix):
    matrix = matrix.astype(jnp.float32)
    return 0.5 * (matrix + jnp.swapaxes(matrix, -1, -2))


def halo(cells, axis):
    count = lax.axis_size(axis)
    ends = count - 1
    below = lax.ppermute(cells[-1:], axis, [(i, i + 1) for i in range(ends)])
    above = lax.ppermute(cells[:1], axis, [(i + 1, i) for i in range(ends)])
    return below, above


def _interior_kernel(r_ref, c_ref, o_ref):
    layers = c_ref.shape[0]
    for layer in range(layers):
        running = None
        for offset in range(3):
            index = layer + offset - 1
            if 0 <= index < layers:
                factor = r_ref[layer, offset]
                left_part = jnp.dot(
                    factor, c_ref[index], preferred_element_type=jnp.float32
                ).astype(jnp.bfloat16)
                term_part = lax.dot_general(
                    left_part,
                    factor,
                    (((1,), (1,)), ((), ())),
                    preferred_element_type=jnp.float32,
                )
                running = term_part if running is None else running + term_part
        o_ref[layer] = running


def _lesser_kernel(part_ref, r_edge_ref, below_ref, above_ref, *rest):
    if len(rest) == 3:
        screen_ref, o_ref, packed_ref = rest
    else:
        screen_ref, (o_ref, packed_ref) = None, rest
    layers = part_ref.shape[0]
    n = part_ref.shape[-1]
    h = n // 2
    rows = lax.broadcasted_iota(jnp.int32, (h, h), 0)
    cols = lax.broadcasted_iota(jnp.int32, (h, h), 1)

    def edge_term(factor, neighbour):
        left_part = jnp.dot(factor, neighbour, preferred_element_type=jnp.float32).astype(
            jnp.bfloat16
        )
        return lax.dot_general(
            left_part, factor, (((1,), (1,)), ((), ())), preferred_element_type=jnp.float32
        )

    for layer in range(layers):
        running = part_ref[layer]
        if layer == 0:
            running = running + edge_term(r_edge_ref[0], below_ref[0])
        if layer == layers - 1:
            running = running + edge_term(r_edge_ref[1], above_ref[0])
        block = (0.5 * (running + running.T)).astype(o_ref.dtype)
        o_ref[layer] = block
        top_left = block[:h, :h]
        bottom_right = block[h:, h:]
        packed_ref[layer, :, :h] = jnp.where(rows <= cols, top_left, bottom_right)
        packed_ref[layer, :, h : 2 * h] = block[:h, h:]
        if screen_ref is None:
            packed_ref[layer, :, 2 * h :] = jnp.where(
                rows == cols, bottom_right, jnp.zeros_like(bottom_right)
            )
        else:
            packed_ref[layer, :, 2 * h : 4 * h] = screen_ref[layer, :, : 2 * h]
            packed_ref[layer, :, 4 * h :] = jnp.where(
                rows == cols, bottom_right, screen_ref[layer, :, 2 * h :]
            )


def lesser_blocks(retarded, coupling, below, above, screen_packed=None):
    layers, n = coupling.shape[0], coupling.shape[-1]
    interior = pl.pallas_call(
        _interior_kernel,
        out_shape=jax.ShapeDtypeStruct(coupling.shape, jnp.float32),
        cost_estimate=pl.CostEstimate(
            flops=(3 * layers - 2) * 4 * n * n * n,
            bytes_accessed=(layers * 3 + layers + layers * 2) * n * n * 2,
            transcendentals=0,
        ),
    )(retarded, coupling)
    edges = jnp.stack([retarded[0, 0], retarded[layers - 1, 2]])
    width = 3 * n // 2 if screen_packed is None else 5 * n // 2
    args = (interior, edges, below, above)
    if screen_packed is not None:
        args = args + (screen_packed,)
    return pl.pallas_call(
        _lesser_kernel,
        out_shape=(
            jax.ShapeDtypeStruct(coupling.shape, jnp.bfloat16),
            jax.ShapeDtypeStruct((layers, n // 2, width), jnp.bfloat16),
        ),
        cost_estimate=pl.CostEstimate(
            flops=2 * 4 * n * n * n,
            bytes_accessed=(layers * 2 + 4 + layers * 2) * n * n * 2,
            transcendentals=0,
        ),
    )(*args)


def _conv_core(lf, sf, o_ref, group=4):
    energies = o_ref.shape[0]
    for first in range(0, energies, group):
        last = min(first + group, energies)
        acc = [None] * (last - first)
        window = {}
        for j in range(last):
            s_row = sf[j]
            for e in range(max(first, j), last):
                if e - j not in window:
                    window[e - j] = lf[e - j]
                term = window[e - j] * s_row
                k = e - first
                acc[k] = term if acc[k] is None else acc[k] + term
            window.pop(last - 1 - j, None)
        for k in range(last - first):
            o_ref[first + k] = acc[k].astype(o_ref.dtype)


def _conv_first_kernel(x_ref, o_ref, s_out_ref, lf, sf):
    energies = o_ref.shape[0]
    h = x_ref.shape[-1] // 5
    for e in range(energies):
        lf[e, :, : 2 * h] = x_ref[e, :, : 2 * h].astype(jnp.float32)
        sf[e, :, : 2 * h] = x_ref[e, :, 2 * h : 4 * h].astype(jnp.float32)
        shared = x_ref[e, :, 4 * h :].astype(jnp.float32)
        lf[e, :, 2 * h :] = shared
        sf[e, :, 2 * h :] = pltpu.roll(shared, h // 2, 1)
    _conv_core(lf, sf, o_ref)
    s_out_ref[...] = sf[...].astype(s_out_ref.dtype)


def _conv_kernel(l_ref, s_ref, o_ref, lf, sf):
    energies = o_ref.shape[0]
    for e in range(energies):
        lf[e] = l_ref[e].astype(jnp.float32)
        sf[e] = s_ref[e].astype(jnp.float32)
    _conv_core(lf, sf, o_ref)


def _conv_call(kernel, outs, block, args):
    energies = block[0]
    elems = block[0] * block[1] * block[2]
    return pl.pallas_call(
        kernel,
        out_shape=outs,
        scratch_shapes=[pltpu.VMEM(block, jnp.float32), pltpu.VMEM(block, jnp.float32)],
        cost_estimate=pl.CostEstimate(
            flops=elems * (energies + 1), bytes_accessed=elems * 8, transcendentals=0
        ),
    )(*args)


def energy_convolve_first(x):
    energies, rows, width = x.shape
    block = (energies, rows, width // 5 * 3)
    outs = (jax.ShapeDtypeStruct(block, jnp.bfloat16), jax.ShapeDtypeStruct(block, jnp.bfloat16))
    return _conv_call(_conv_first_kernel, outs, block, (x,))


def energy_convolve(l_arr, s_arr):
    block = l_arr.shape
    return _conv_call(_conv_kernel, jax.ShapeDtypeStruct(block, jnp.bfloat16), block, (l_arr, s_arr))


def pack_symmetric(blocks):
    half = blocks.shape[-1] // 2
    rows = lax.broadcasted_iota(jnp.int32, (half, half), 0)
    cols = lax.broadcasted_iota(jnp.int32, (half, half), 1)
    top_left = blocks[:, :half, :half]
    bottom_right = blocks[:, half:, half:]
    folded = jnp.where(rows <= cols, top_left, bottom_right)
    diagonal = jnp.where(rows == cols, bottom_right, jnp.zeros_like(bottom_right))
    return jnp.concatenate([folded, blocks[:, :half, half:], diagonal], axis=-1)


def pack_screened(blocks):
    half = blocks.shape[-1] // 2
    packed = pack_symmetric(blocks)
    moved = jnp.roll(packed[..., 2 * half :], half // 2, axis=-1)
    return jnp.concatenate([packed[..., : 2 * half], moved], axis=-1)


def unpack_symmetric(packed):
    half = packed.shape[-1] // 3
    rows = lax.broadcasted_iota(jnp.int32, (half, half), 0)
    cols = lax.broadcasted_iota(jnp.int32, (half, half), 1)
    folded = packed[..., :half]
    off = packed[..., half : 2 * half]
    diagonal = packed[..., 2 * half :]
    flipped = jnp.swapaxes(folded, -1, -2)
    top_left = jnp.where(rows <= cols, folded, flipped)
    bottom_right = jnp.where(rows > cols, folded, flipped)
    bottom_right = jnp.where(rows == cols, diagonal, bottom_right)
    top = jnp.concatenate([top_left, off], axis=-1)
    bottom = jnp.concatenate([jnp.swapaxes(off, -1, -2), bottom_right], axis=-1)
    return jnp.concatenate([top, bottom], axis=-2)


def shards(retarded, scatter_in, screen):
    energies = lax.axis_size("energy")
    layers = retarded.shape[1]
    orbitals = retarded.shape[-1]
    half = orbitals // 2
    rows = layers * half // energies
    retarded = retarded[0]
    base_part = symmetric(scatter_in[0])
    screened = symmetric(screen[0]).astype(jnp.bfloat16)

    def to_blocks(columns):
        return unpack_symmetric(columns.reshape(layers, half, columns.shape[-1]))

    correction = None
    screen_columns = None
    lesser = None
    self_energy = None
    for iteration in range(ITERS):
        if correction is None:
            coupling = base_part.astype(jnp.bfloat16)
        else:
            coupling = (base_part + correction).astype(jnp.bfloat16)
        below, above = halo(coupling, "layer")
        if screen_columns is None:
            lesser, both = lesser_blocks(retarded, coupling, below, above, pack_screened(screened))
            both = lax.all_to_all(
                both.reshape(energies, rows, both.shape[-1]), "energy", 0, 0, tiled=True
            )
            self_columns, screen_columns = energy_convolve_first(both)
        else:
            lesser, packed = lesser_blocks(retarded, coupling, below, above)
            lesser_columns = lax.all_to_all(
                packed.reshape(energies, rows, packed.shape[-1]), "energy", 0, 0, tiled=True
            )
            self_columns = energy_convolve(lesser_columns, screen_columns)
        returned = lax.all_to_all(self_columns, "energy", 0, 0, tiled=True)
        self_blocks = to_blocks(returned)
        self_energy = self_blocks[None]
        correction = self_blocks.astype(jnp.float32)
    return (lesser[None], self_energy)


def solution(mesh):
    placed = (
        P("energy", "layer", None, None, None),
        P("energy", "layer", None, None),
        P("energy", "layer", None, None),
    )
    return jax.shard_map(
        shards,
        mesh=mesh,
        in_specs=placed,
        out_specs=(P("energy", "layer", None, None), P("energy", "layer", None, None)),
        check_vma=False,
    )
```

```python
import functools

import jax
import jax.numpy as jnp
from jax import lax
from jax.experimental import pallas as pl
from jax.experimental.pallas import tpu as pltpu
from jax.sharding import PartitionSpec as P

ITERS = 2


def symmetric(matrix):
    matrix = matrix.astype(jnp.float32)
    return 0.5 * (matrix + jnp.swapaxes(matrix, -1, -2))


def halo(cells, axis):
    count = lax.axis_size(axis)
    ends = count - 1
    below = lax.ppermute(cells[-1:], axis, [(i, i + 1) for i in range(ends)])
    above = lax.ppermute(cells[:1], axis, [(i + 1, i) for i in range(ends)])
    return below, above


def _lesser_kernel(r_ref, c_ref, below_ref, above_ref, *rest):
    if len(rest) == 3:
        screen_ref, o_ref, packed_ref = rest
    else:
        screen_ref, (o_ref, packed_ref) = None, rest
    layers = c_ref.shape[0]
    n = c_ref.shape[-1]
    h = n // 2
    layer = pl.program_id(0)
    rows = lax.broadcasted_iota(jnp.int32, (h, h), 0)
    cols = lax.broadcasted_iota(jnp.int32, (h, h), 1)
    neighbours = (
        jnp.where(layer == 0, below_ref[0], c_ref[jnp.maximum(layer - 1, 0)]),
        c_ref[layer],
        jnp.where(layer == layers - 1, above_ref[0], c_ref[jnp.minimum(layer + 1, layers - 1)]),
    )
    running = None
    for offset in range(3):
        factor = r_ref[0, offset]
        left_part = jnp.dot(
            factor, neighbours[offset], preferred_element_type=jnp.float32
        ).astype(jnp.bfloat16)
        term_part = lax.dot_general(
            left_part,
            factor,
            (((1,), (1,)), ((), ())),
            preferred_element_type=jnp.float32,
        )
        running = term_part if running is None else running + term_part
    block = (0.5 * (running + running.T)).astype(o_ref.dtype)
    o_ref[0] = block
    top_left = block[:h, :h]
    bottom_right = block[h:, h:]
    packed_ref[0, :, :h] = jnp.where(rows <= cols, top_left, bottom_right)
    packed_ref[0, :, h : 2 * h] = block[:h, h:]
    if screen_ref is None:
        packed_ref[0, :, 2 * h :] = jnp.where(
            rows == cols, bottom_right, jnp.zeros_like(bottom_right)
        )
    else:
        packed_ref[0, :, 2 * h : 4 * h] = screen_ref[0, :, : 2 * h]
        packed_ref[0, :, 4 * h :] = jnp.where(
            rows == cols, bottom_right, screen_ref[0, :, 2 * h :]
        )


def lesser_blocks(retarded, coupling, below, above, screen_packed=None):
    layers, n = coupling.shape[0], coupling.shape[-1]
    h = n // 2
    width = 3 * n // 2 if screen_packed is None else 5 * n // 2
    args = (retarded, coupling, below, above)
    in_specs = [
        pl.BlockSpec((1, 3, n, n), lambda l: (l, 0, 0, 0)),
        pl.BlockSpec((layers, n, n), lambda l: (0, 0, 0)),
        pl.BlockSpec((1, n, n), lambda l: (0, 0, 0)),
        pl.BlockSpec((1, n, n), lambda l: (0, 0, 0)),
    ]
    if screen_packed is not None:
        args = args + (screen_packed,)
        in_specs.append(pl.BlockSpec((1, h, 3 * h), lambda l: (l, 0, 0)))
    return pl.pallas_call(
        _lesser_kernel,
        grid=(layers,),
        in_specs=in_specs,
        out_specs=(
            pl.BlockSpec((1, n, n), lambda l: (l, 0, 0)),
            pl.BlockSpec((1, h, width), lambda l: (l, 0, 0)),
        ),
        out_shape=(
            jax.ShapeDtypeStruct(coupling.shape, jnp.bfloat16),
            jax.ShapeDtypeStruct((layers, h, width), jnp.bfloat16),
        ),
        cost_estimate=pl.CostEstimate(
            flops=layers * 3 * 4 * n * n * n,
            bytes_accessed=(layers * 3 + layers + 2 + layers * 2) * n * n * 2,
            transcendentals=0,
        ),
    )(*args)


def _conv_core(lf, sf, o_ref, group=4):
    energies = o_ref.shape[0]
    for first in range(0, energies, group):
        last = min(first + group, energies)
        acc = [None] * (last - first)
        window = {}
        for j in range(last):
            s_row = sf[j]
            for e in range(max(first, j), last):
                if e - j not in window:
                    window[e - j] = lf[e - j]
                term = window[e - j] * s_row
                k = e - first
                acc[k] = term if acc[k] is None else acc[k] + term
            window.pop(last - 1 - j, None)
        for k in range(last - first):
            o_ref[first + k] = acc[k].astype(o_ref.dtype)


def _conv_first_kernel(x_ref, o_ref, s_out_ref, lf, sf):
    energies = o_ref.shape[0]
    h = x_ref.shape[-1] // 5
    for e in range(energies):
        lf[e, :, : 2 * h] = x_ref[e, :, : 2 * h].astype(jnp.float32)
        sf[e, :, : 2 * h] = x_ref[e, :, 2 * h : 4 * h].astype(jnp.float32)
        shared = x_ref[e, :, 4 * h :].astype(jnp.float32)
        lf[e, :, 2 * h :] = shared
        sf[e, :, 2 * h :] = pltpu.roll(shared, h // 2, 1)
    _conv_core(lf, sf, o_ref)
    s_out_ref[...] = sf[...].astype(s_out_ref.dtype)


def _conv_kernel(l_ref, s_ref, o_ref, lf, sf):
    energies = o_ref.shape[0]
    for e in range(energies):
        lf[e] = l_ref[e].astype(jnp.float32)
        sf[e] = s_ref[e].astype(jnp.float32)
    _conv_core(lf, sf, o_ref)


def _conv_call(kernel, outs, block, args):
    energies = block[0]
    elems = block[0] * block[1] * block[2]
    return pl.pallas_call(
        kernel,
        out_shape=outs,
        scratch_shapes=[pltpu.VMEM(block, jnp.float32), pltpu.VMEM(block, jnp.float32)],
        cost_estimate=pl.CostEstimate(
            flops=elems * (energies + 1), bytes_accessed=elems * 8, transcendentals=0
        ),
    )(*args)


def energy_convolve_first(x):
    energies, rows, width = x.shape
    block = (energies, rows, width // 5 * 3)
    outs = (jax.ShapeDtypeStruct(block, jnp.bfloat16), jax.ShapeDtypeStruct(block, jnp.bfloat16))
    return _conv_call(_conv_first_kernel, outs, block, (x,))


def energy_convolve(l_arr, s_arr):
    block = l_arr.shape
    return _conv_call(_conv_kernel, jax.ShapeDtypeStruct(block, jnp.bfloat16), block, (l_arr, s_arr))


def pack_symmetric(blocks):
    half = blocks.shape[-1] // 2
    rows = lax.broadcasted_iota(jnp.int32, (half, half), 0)
    cols = lax.broadcasted_iota(jnp.int32, (half, half), 1)
    top_left = blocks[:, :half, :half]
    bottom_right = blocks[:, half:, half:]
    folded = jnp.where(rows <= cols, top_left, bottom_right)
    diagonal = jnp.where(rows == cols, bottom_right, jnp.zeros_like(bottom_right))
    return jnp.concatenate([folded, blocks[:, :half, half:], diagonal], axis=-1)


def pack_screened(blocks):
    half = blocks.shape[-1] // 2
    packed = pack_symmetric(blocks)
    moved = jnp.roll(packed[..., 2 * half :], half // 2, axis=-1)
    return jnp.concatenate([packed[..., : 2 * half], moved], axis=-1)


def unpack_symmetric(packed):
    half = packed.shape[-1] // 3
    rows = lax.broadcasted_iota(jnp.int32, (half, half), 0)
    cols = lax.broadcasted_iota(jnp.int32, (half, half), 1)
    folded = packed[..., :half]
    off = packed[..., half : 2 * half]
    diagonal = packed[..., 2 * half :]
    flipped = jnp.swapaxes(folded, -1, -2)
    top_left = jnp.where(rows <= cols, folded, flipped)
    bottom_right = jnp.where(rows > cols, folded, flipped)
    bottom_right = jnp.where(rows == cols, diagonal, bottom_right)
    top = jnp.concatenate([top_left, off], axis=-1)
    bottom = jnp.concatenate([jnp.swapaxes(off, -1, -2), bottom_right], axis=-1)
    return jnp.concatenate([top, bottom], axis=-2)


def shards(retarded, scatter_in, screen):
    energies = lax.axis_size("energy")
    layers = retarded.shape[1]
    orbitals = retarded.shape[-1]
    half = orbitals // 2
    rows = layers * half // energies
    retarded = retarded[0]
    base_part = symmetric(scatter_in[0])
    screened = symmetric(screen[0]).astype(jnp.bfloat16)

    def to_blocks(columns):
        return unpack_symmetric(columns.reshape(layers, half, columns.shape[-1]))

    correction = None
    screen_columns = None
    lesser = None
    self_energy = None
    for iteration in range(ITERS):
        if correction is None:
            coupling = base_part.astype(jnp.bfloat16)
        else:
            coupling = (base_part + correction).astype(jnp.bfloat16)
        below, above = halo(coupling, "layer")
        if screen_columns is None:
            lesser, both = lesser_blocks(retarded, coupling, below, above, pack_screened(screened))
            both = lax.all_to_all(
                both.reshape(energies, rows, both.shape[-1]), "energy", 0, 0, tiled=True
            )
            self_columns, screen_columns = energy_convolve_first(both)
        else:
            lesser, packed = lesser_blocks(retarded, coupling, below, above)
            lesser_columns = lax.all_to_all(
                packed.reshape(energies, rows, packed.shape[-1]), "energy", 0, 0, tiled=True
            )
            self_columns = energy_convolve(lesser_columns, screen_columns)
        returned = lax.all_to_all(self_columns, "energy", 0, 0, tiled=True)
        self_blocks = to_blocks(returned)
        self_energy = self_blocks[None]
        correction = self_blocks.astype(jnp.float32)
    return (lesser[None], self_energy)


def solution(mesh):
    placed = (
        P("energy", "layer", None, None, None),
        P("energy", "layer", None, None),
        P("energy", "layer", None, None),
    )
    return jax.shard_map(
        shards,
        mesh=mesh,
        in_specs=placed,
        out_specs=(P("energy", "layer", None, None), P("energy", "layer", None, None)),
        check_vma=False,
    )
```

```python
import functools

import jax
import jax.numpy as jnp
from jax import lax
from jax.experimental import pallas as pl
from jax.experimental.pallas import tpu as pltpu
from jax.sharding import PartitionSpec as P

ITERS = 2


def symmetric(matrix):
    matrix = matrix.astype(jnp.float32)
    return 0.5 * (matrix + jnp.swapaxes(matrix, -1, -2))


def halo(cells, axis):
    count = lax.axis_size(axis)
    ends = count - 1
    below = lax.ppermute(cells[-1:], axis, [(i, i + 1) for i in range(ends)])
    above = lax.ppermute(cells[:1], axis, [(i + 1, i) for i in range(ends)])
    return below, above


def _lesser_kernel(r_ref, c_ref, below_ref, above_ref, *rest):
    if len(rest) == 3:
        screen_ref, o_ref, packed_ref = rest
    else:
        screen_ref, (o_ref, packed_ref) = None, rest
    layers = c_ref.shape[0]
    n = c_ref.shape[-1]
    h = n // 2
    rows = lax.broadcasted_iota(jnp.int32, (h, h), 0)
    cols = lax.broadcasted_iota(jnp.int32, (h, h), 1)

    def neighbour(index):
        if index < 0:
            return below_ref[0]
        if index >= layers:
            return above_ref[0]
        return c_ref[index]

    for layer in range(layers):
        running = None
        for offset in range(3):
            factor = r_ref[layer, offset]
            left_part = jnp.dot(
                factor, neighbour(layer + offset - 1), preferred_element_type=jnp.float32
            ).astype(jnp.bfloat16)
            term_part = lax.dot_general(
                left_part,
                factor,
                (((1,), (1,)), ((), ())),
                preferred_element_type=jnp.float32,
            )
            running = term_part if running is None else running + term_part
        block = (0.5 * (running + running.T)).astype(o_ref.dtype)
        o_ref[layer] = block
        top_left = block[:h, :h]
        bottom_right = block[h:, h:]
        packed_ref[layer, :, :h] = jnp.where(rows <= cols, top_left, bottom_right)
        packed_ref[layer, :, h : 2 * h] = block[:h, h:]
        if screen_ref is None:
            packed_ref[layer, :, 2 * h :] = jnp.where(
                rows == cols, bottom_right, jnp.zeros_like(bottom_right)
            )
        else:
            packed_ref[layer, :, 2 * h : 4 * h] = screen_ref[layer, :, : 2 * h]
            packed_ref[layer, :, 4 * h :] = jnp.where(
                rows == cols, bottom_right, screen_ref[layer, :, 2 * h :]
            )


def lesser_blocks(retarded, coupling, below, above, screen_packed=None):
    layers, n = coupling.shape[0], coupling.shape[-1]
    width = 3 * n // 2 if screen_packed is None else 5 * n // 2
    args = (retarded, coupling, below, above)
    if screen_packed is not None:
        args = args + (screen_packed,)
    return pl.pallas_call(
        _lesser_kernel,
        out_shape=(
            jax.ShapeDtypeStruct(coupling.shape, jnp.bfloat16),
            jax.ShapeDtypeStruct((layers, n // 2, width), jnp.bfloat16),
        ),
        cost_estimate=pl.CostEstimate(
            flops=layers * 3 * 4 * n * n * n,
            bytes_accessed=(layers * 3 + layers + 2 + layers * 2) * n * n * 2,
            transcendentals=0,
        ),
    )(*args)


def _conv_core(lf, sf, o_ref, group=8):
    energies = o_ref.shape[0]
    for first in range(0, energies, group):
        last = min(first + group, energies)
        acc = [None] * (last - first)
        window = {}
        for j in range(last):
            s_row = sf[j]
            for e in range(max(first, j), last):
                if e - j not in window:
                    window[e - j] = lf[e - j]
                term = window[e - j] * s_row
                k = e - first
                acc[k] = term if acc[k] is None else acc[k] + term
            window.pop(last - 1 - j, None)
        for k in range(last - first):
            o_ref[first + k] = acc[k].astype(o_ref.dtype)


def _conv_first_kernel(x_ref, o_ref, s_out_ref, lf, sf):
    energies = o_ref.shape[0]
    h = x_ref.shape[-1] // 5
    for e in range(energies):
        lf[e, :, : 2 * h] = x_ref[e, :, : 2 * h].astype(jnp.float32)
        sf[e, :, : 2 * h] = x_ref[e, :, 2 * h : 4 * h].astype(jnp.float32)
        shared = x_ref[e, :, 4 * h :].astype(jnp.float32)
        lf[e, :, 2 * h :] = shared
        sf[e, :, 2 * h :] = pltpu.roll(shared, h // 2, 1)
    _conv_core(lf, sf, o_ref)
    s_out_ref[...] = sf[...].astype(s_out_ref.dtype)


def _conv_kernel(l_ref, s_ref, o_ref, lf, sf):
    energies = o_ref.shape[0]
    for e in range(energies):
        lf[e] = l_ref[e].astype(jnp.float32)
        sf[e] = s_ref[e].astype(jnp.float32)
    _conv_core(lf, sf, o_ref)


def _conv_call(kernel, outs, block, args):
    energies = block[0]
    elems = block[0] * block[1] * block[2]
    return pl.pallas_call(
        kernel,
        out_shape=outs,
        scratch_shapes=[pltpu.VMEM(block, jnp.float32), pltpu.VMEM(block, jnp.float32)],
        cost_estimate=pl.CostEstimate(
            flops=elems * (energies + 1), bytes_accessed=elems * 8, transcendentals=0
        ),
    )(*args)


def energy_convolve_first(x):
    energies, rows, width = x.shape
    block = (energies, rows, width // 5 * 3)
    outs = (jax.ShapeDtypeStruct(block, jnp.bfloat16), jax.ShapeDtypeStruct(block, jnp.bfloat16))
    return _conv_call(_conv_first_kernel, outs, block, (x,))


def energy_convolve(l_arr, s_arr):
    block = l_arr.shape
    return _conv_call(_conv_kernel, jax.ShapeDtypeStruct(block, jnp.bfloat16), block, (l_arr, s_arr))


def pack_symmetric(blocks):
    half = blocks.shape[-1] // 2
    rows = lax.broadcasted_iota(jnp.int32, (half, half), 0)
    cols = lax.broadcasted_iota(jnp.int32, (half, half), 1)
    top_left = blocks[:, :half, :half]
    bottom_right = blocks[:, half:, half:]
    folded = jnp.where(rows <= cols, top_left, bottom_right)
    diagonal = jnp.where(rows == cols, bottom_right, jnp.zeros_like(bottom_right))
    return jnp.concatenate([folded, blocks[:, :half, half:], diagonal], axis=-1)


def pack_screened(blocks):
    half = blocks.shape[-1] // 2
    packed = pack_symmetric(blocks)
    moved = jnp.roll(packed[..., 2 * half :], half // 2, axis=-1)
    return jnp.concatenate([packed[..., : 2 * half], moved], axis=-1)


def unpack_symmetric(packed):
    half = packed.shape[-1] // 3
    rows = lax.broadcasted_iota(jnp.int32, (half, half), 0)
    cols = lax.broadcasted_iota(jnp.int32, (half, half), 1)
    folded = packed[..., :half]
    off = packed[..., half : 2 * half]
    diagonal = packed[..., 2 * half :]
    flipped = jnp.swapaxes(folded, -1, -2)
    top_left = jnp.where(rows <= cols, folded, flipped)
    bottom_right = jnp.where(rows > cols, folded, flipped)
    bottom_right = jnp.where(rows == cols, diagonal, bottom_right)
    top = jnp.concatenate([top_left, off], axis=-1)
    bottom = jnp.concatenate([jnp.swapaxes(off, -1, -2), bottom_right], axis=-1)
    return jnp.concatenate([top, bottom], axis=-2)


def shards(retarded, scatter_in, screen):
    energies = lax.axis_size("energy")
    layers = retarded.shape[1]
    orbitals = retarded.shape[-1]
    half = orbitals // 2
    rows = layers * half // energies
    retarded = retarded[0]
    base_part = symmetric(scatter_in[0])
    screened = symmetric(screen[0]).astype(jnp.bfloat16)

    def to_blocks(columns):
        return unpack_symmetric(columns.reshape(layers, half, columns.shape[-1]))

    correction = None
    screen_columns = None
    lesser = None
    self_energy = None
    for iteration in range(ITERS):
        if correction is None:
            coupling = base_part.astype(jnp.bfloat16)
        else:
            coupling = (base_part + correction).astype(jnp.bfloat16)
        below, above = halo(coupling, "layer")
        if screen_columns is None:
            lesser, both = lesser_blocks(retarded, coupling, below, above, pack_screened(screened))
            both = lax.all_to_all(
                both.reshape(energies, rows, both.shape[-1]), "energy", 0, 0, tiled=True
            )
            self_columns, screen_columns = energy_convolve_first(both)
        else:
            lesser, packed = lesser_blocks(retarded, coupling, below, above)
            lesser_columns = lax.all_to_all(
                packed.reshape(energies, rows, packed.shape[-1]), "energy", 0, 0, tiled=True
            )
            self_columns = energy_convolve(lesser_columns, screen_columns)
        returned = lax.all_to_all(self_columns, "energy", 0, 0, tiled=True)
        self_blocks = to_blocks(returned)
        self_energy = self_blocks[None]
        correction = self_blocks.astype(jnp.float32)
    return (lesser[None], self_energy)


def solution(mesh):
    placed = (
        P("energy", "layer", None, None, None),
        P("energy", "layer", None, None),
        P("energy", "layer", None, None),
    )
    return jax.shard_map(
        shards,
        mesh=mesh,
        in_specs=placed,
        out_specs=(P("energy", "layer", None, None), P("energy", "layer", None, None)),
        check_vma=False,
    )
```

```python
import functools

import jax
import jax.numpy as jnp
from jax import lax
from jax.experimental import pallas as pl
from jax.experimental.pallas import tpu as pltpu
from jax.sharding import PartitionSpec as P

ITERS = 2


def symmetric(matrix):
    matrix = matrix.astype(jnp.float32)
    return 0.5 * (matrix + jnp.swapaxes(matrix, -1, -2))


def halo(cells, axis):
    count = lax.axis_size(axis)
    ends = count - 1
    below = lax.ppermute(cells[-1:], axis, [(i, i + 1) for i in range(ends)])
    above = lax.ppermute(cells[:1], axis, [(i + 1, i) for i in range(ends)])
    return below, above


def _lesser_kernel(r_ref, s_ref, corr_ref, below_ref, above_ref, *rest):
    if len(rest) == 3:
        screen_ref, o_ref, packed_ref = rest
    else:
        screen_ref, (o_ref, packed_ref) = None, rest
    layers = s_ref.shape[0]
    n = s_ref.shape[-1]
    h = n // 2
    rows = lax.broadcasted_iota(jnp.int32, (h, h), 0)
    cols = lax.broadcasted_iota(jnp.int32, (h, h), 1)
    couplings = []
    for layer in range(layers):
        raw = s_ref[layer].astype(jnp.float32)
        base = 0.5 * (raw + raw.T)
        if corr_ref is not None:
            base = base + corr_ref[layer].astype(jnp.float32)
        couplings.append(base.astype(jnp.bfloat16))

    def neighbour(index):
        if index < 0:
            return below_ref[0]
        if index >= layers:
            return above_ref[0]
        return couplings[index]

    for layer in range(layers):
        running = None
        for offset in range(3):
            factor = r_ref[layer, offset]
            left_part = jnp.dot(
                factor, neighbour(layer + offset - 1), preferred_element_type=jnp.float32
            ).astype(jnp.bfloat16)
            term_part = lax.dot_general(
                left_part,
                factor,
                (((1,), (1,)), ((), ())),
                preferred_element_type=jnp.float32,
            )
            running = term_part if running is None else running + term_part
        block = (0.5 * (running + running.T)).astype(o_ref.dtype)
        o_ref[layer] = block
        top_left = block[:h, :h]
        bottom_right = block[h:, h:]
        packed_ref[layer, :, :h] = jnp.where(rows <= cols, top_left, bottom_right)
        packed_ref[layer, :, h : 2 * h] = block[:h, h:]
        if screen_ref is None:
            packed_ref[layer, :, 2 * h :] = jnp.where(
                rows == cols, bottom_right, jnp.zeros_like(bottom_right)
            )
        else:
            packed_ref[layer, :, 2 * h : 4 * h] = screen_ref[layer, :, : 2 * h]
            packed_ref[layer, :, 4 * h :] = jnp.where(
                rows == cols, bottom_right, screen_ref[layer, :, 2 * h :]
            )


def lesser_blocks(retarded, scatter, correction, below, above, screen_packed=None):
    layers, n = scatter.shape[0], scatter.shape[-1]
    width = 3 * n // 2 if screen_packed is None else 5 * n // 2
    args = [retarded, scatter] + ([] if correction is None else [correction]) + [below, above]
    if screen_packed is not None:
        args.append(screen_packed)

    def kernel(*refs):
        if correction is None:
            refs = refs[:2] + (None,) + refs[2:]
        _lesser_kernel(*refs)

    return pl.pallas_call(
        kernel,
        out_shape=(
            jax.ShapeDtypeStruct(scatter.shape, jnp.bfloat16),
            jax.ShapeDtypeStruct((layers, n // 2, width), jnp.bfloat16),
        ),
        cost_estimate=pl.CostEstimate(
            flops=layers * 3 * 4 * n * n * n,
            bytes_accessed=(layers * 3 + layers * 2 + 2 + layers * 2) * n * n * 2,
            transcendentals=0,
        ),
    )(*args)


def _conv_core(lf, sf, o_ref, group=4):
    energies = o_ref.shape[0]
    for first in range(0, energies, group):
        last = min(first + group, energies)
        acc = [None] * (last - first)
        window = {}
        for j in range(last):
            s_row = sf[j]
            for e in range(max(first, j), last):
                if e - j not in window:
                    window[e - j] = lf[e - j]
                term = window[e - j] * s_row
                k = e - first
                acc[k] = term if acc[k] is None else acc[k] + term
            window.pop(last - 1 - j, None)
        for k in range(last - first):
            o_ref[first + k] = acc[k].astype(o_ref.dtype)


def _conv_first_kernel(x_ref, o_ref, s_out_ref, lf, sf):
    energies = o_ref.shape[0]
    h = x_ref.shape[-1] // 5
    for e in range(energies):
        lf[e, :, : 2 * h] = x_ref[e, :, : 2 * h].astype(jnp.float32)
        sf[e, :, : 2 * h] = x_ref[e, :, 2 * h : 4 * h].astype(jnp.float32)
        shared = x_ref[e, :, 4 * h :].astype(jnp.float32)
        lf[e, :, 2 * h :] = shared
        sf[e, :, 2 * h :] = pltpu.roll(shared, h // 2, 1)
    _conv_core(lf, sf, o_ref)
    s_out_ref[...] = sf[...].astype(s_out_ref.dtype)


def _conv_kernel(l_ref, s_ref, o_ref, lf, sf):
    energies = o_ref.shape[0]
    for e in range(energies):
        lf[e] = l_ref[e].astype(jnp.float32)
        sf[e] = s_ref[e].astype(jnp.float32)
    _conv_core(lf, sf, o_ref)


def _conv_call(kernel, outs, block, args):
    energies = block[0]
    elems = block[0] * block[1] * block[2]
    return pl.pallas_call(
        kernel,
        out_shape=outs,
        scratch_shapes=[pltpu.VMEM(block, jnp.float32), pltpu.VMEM(block, jnp.float32)],
        cost_estimate=pl.CostEstimate(
            flops=elems * (energies + 1), bytes_accessed=elems * 8, transcendentals=0
        ),
    )(*args)


def energy_convolve_first(x):
    energies, rows, width = x.shape
    block = (energies, rows, width // 5 * 3)
    outs = (jax.ShapeDtypeStruct(block, jnp.bfloat16), jax.ShapeDtypeStruct(block, jnp.bfloat16))
    return _conv_call(_conv_first_kernel, outs, block, (x,))


def energy_convolve(l_arr, s_arr):
    block = l_arr.shape
    return _conv_call(_conv_kernel, jax.ShapeDtypeStruct(block, jnp.bfloat16), block, (l_arr, s_arr))


def pack_symmetric(blocks):
    half = blocks.shape[-1] // 2
    rows = lax.broadcasted_iota(jnp.int32, (half, half), 0)
    cols = lax.broadcasted_iota(jnp.int32, (half, half), 1)
    top_left = blocks[:, :half, :half]
    bottom_right = blocks[:, half:, half:]
    folded = jnp.where(rows <= cols, top_left, bottom_right)
    diagonal = jnp.where(rows == cols, bottom_right, jnp.zeros_like(bottom_right))
    return jnp.concatenate([folded, blocks[:, :half, half:], diagonal], axis=-1)


def pack_screened(blocks):
    half = blocks.shape[-1] // 2
    packed = pack_symmetric(blocks)
    moved = jnp.roll(packed[..., 2 * half :], half // 2, axis=-1)
    return jnp.concatenate([packed[..., : 2 * half], moved], axis=-1)


def unpack_symmetric(packed):
    half = packed.shape[-1] // 3
    rows = lax.broadcasted_iota(jnp.int32, (half, half), 0)
    cols = lax.broadcasted_iota(jnp.int32, (half, half), 1)
    folded = packed[..., :half]
    off = packed[..., half : 2 * half]
    diagonal = packed[..., 2 * half :]
    flipped = jnp.swapaxes(folded, -1, -2)
    top_left = jnp.where(rows <= cols, folded, flipped)
    bottom_right = jnp.where(rows > cols, folded, flipped)
    bottom_right = jnp.where(rows == cols, diagonal, bottom_right)
    top = jnp.concatenate([top_left, off], axis=-1)
    bottom = jnp.concatenate([jnp.swapaxes(off, -1, -2), bottom_right], axis=-1)
    return jnp.concatenate([top, bottom], axis=-2)


def shards(retarded, scatter_in, screen):
    energies = lax.axis_size("energy")
    layers = retarded.shape[1]
    orbitals = retarded.shape[-1]
    half = orbitals // 2
    rows = layers * half // energies
    retarded = retarded[0]
    screened = symmetric(screen[0]).astype(jnp.bfloat16)

    def to_blocks(columns):
        return unpack_symmetric(columns.reshape(layers, half, columns.shape[-1]))

    scatter = scatter_in[0]
    correction = None
    screen_columns = None
    lesser = None
    self_energy = None
    for iteration in range(ITERS):
        edges = symmetric(jnp.concatenate([scatter[-1:], scatter[:1]], axis=0))
        if correction is not None:
            edges = edges + jnp.concatenate([correction[-1:], correction[:1]], axis=0).astype(
                jnp.float32
            )
        edges = edges.astype(jnp.bfloat16)
        below, above = halo(jnp.concatenate([edges[1:], edges[:1]], axis=0), "layer")
        if screen_columns is None:
            lesser, both = lesser_blocks(
                retarded, scatter, None, below, above, pack_screened(screened)
            )
            both = lax.all_to_all(
                both.reshape(energies, rows, both.shape[-1]), "energy", 0, 0, tiled=True
            )
            self_columns, screen_columns = energy_convolve_first(both)
        else:
            lesser, packed = lesser_blocks(retarded, scatter, correction, below, above)
            lesser_columns = lax.all_to_all(
                packed.reshape(energies, rows, packed.shape[-1]), "energy", 0, 0, tiled=True
            )
            self_columns = energy_convolve(lesser_columns, screen_columns)
        returned = lax.all_to_all(self_columns, "energy", 0, 0, tiled=True)
        self_blocks = to_blocks(returned)
        self_energy = self_blocks[None]
        correction = self_blocks
    return (lesser[None], self_energy)


def solution(mesh):
    placed = (
        P("energy", "layer", None, None, None),
        P("energy", "layer", None, None),
        P("energy", "layer", None, None),
    )
    return jax.shard_map(
        shards,
        mesh=mesh,
        in_specs=placed,
        out_specs=(P("energy", "layer", None, None), P("energy", "layer", None, None)),
        check_vma=False,
    )
```

```python
import functools

import jax
import jax.numpy as jnp
from jax import lax
from jax.experimental import pallas as pl
from jax.experimental.pallas import tpu as pltpu
from jax.sharding import PartitionSpec as P

ITERS = 2


def symmetric(matrix):
    matrix = matrix.astype(jnp.float32)
    return 0.5 * (matrix + jnp.swapaxes(matrix, -1, -2))


def halo(cells, axis):
    count = lax.axis_size(axis)
    ends = count - 1
    below = lax.ppermute(cells[-1:], axis, [(i, i + 1) for i in range(ends)])
    above = lax.ppermute(cells[:1], axis, [(i + 1, i) for i in range(ends)])
    return below, above


def _lesser_kernel(r_ref, s_ref, corr_ref, below_ref, above_ref, *rest):
    if len(rest) == 3:
        screen_ref, o_ref, packed_ref = rest
    else:
        screen_ref, (o_ref, packed_ref) = None, rest
    layers = s_ref.shape[0]
    n = s_ref.shape[-1]
    h = n // 2
    rows = lax.broadcasted_iota(jnp.int32, (h, h), 0)
    cols = lax.broadcasted_iota(jnp.int32, (h, h), 1)
    couplings = []
    for layer in range(layers):
        raw = s_ref[layer].astype(jnp.float32)
        base = 0.5 * (raw + raw.T)
        if corr_ref is not None:
            packed = corr_ref[layer]
            folded = packed[:, :h]
            off = packed[:, h : 2 * h]
            flipped = folded.T
            top_left = jnp.where(rows <= cols, folded, flipped)
            bottom_right = jnp.where(
                rows == cols, packed[:, 2 * h :], jnp.where(rows > cols, folded, flipped)
            )
            full = jnp.concatenate(
                [
                    jnp.concatenate([top_left, off], axis=1),
                    jnp.concatenate([off.T, bottom_right], axis=1),
                ],
                axis=0,
            )
            base = base + full.astype(jnp.float32)
        couplings.append(base.astype(jnp.bfloat16))

    def neighbour(index):
        if index < 0:
            return below_ref[0]
        if index >= layers:
            return above_ref[0]
        return couplings[index]

    for layer in range(layers):
        running = None
        for offset in range(3):
            factor = r_ref[layer, offset]
            left_part = jnp.dot(
                factor, neighbour(layer + offset - 1), preferred_element_type=jnp.float32
            ).astype(jnp.bfloat16)
            term_part = lax.dot_general(
                left_part,
                factor,
                (((1,), (1,)), ((), ())),
                preferred_element_type=jnp.float32,
            )
            running = term_part if running is None else running + term_part
        block = (0.5 * (running + running.T)).astype(o_ref.dtype)
        o_ref[layer] = block
        top_left = block[:h, :h]
        bottom_right = block[h:, h:]
        packed_ref[layer, :, :h] = jnp.where(rows <= cols, top_left, bottom_right)
        packed_ref[layer, :, h : 2 * h] = block[:h, h:]
        if screen_ref is None:
            packed_ref[layer, :, 2 * h :] = jnp.where(
                rows == cols, bottom_right, jnp.zeros_like(bottom_right)
            )
        else:
            packed_ref[layer, :, 2 * h : 4 * h] = screen_ref[layer, :, : 2 * h]
            packed_ref[layer, :, 4 * h :] = jnp.where(
                rows == cols, bottom_right, screen_ref[layer, :, 2 * h :]
            )


def lesser_blocks(retarded, scatter, correction, below, above, screen_packed=None):
    layers, n = scatter.shape[0], scatter.shape[-1]
    width = 3 * n // 2 if screen_packed is None else 5 * n // 2
    args = [retarded, scatter] + ([] if correction is None else [correction]) + [below, above]
    if screen_packed is not None:
        args.append(screen_packed)

    def kernel(*refs):
        if correction is None:
            refs = refs[:2] + (None,) + refs[2:]
        _lesser_kernel(*refs)

    return pl.pallas_call(
        kernel,
        out_shape=(
            jax.ShapeDtypeStruct(scatter.shape, jnp.bfloat16),
            jax.ShapeDtypeStruct((layers, n // 2, width), jnp.bfloat16),
        ),
        cost_estimate=pl.CostEstimate(
            flops=layers * 3 * 4 * n * n * n,
            bytes_accessed=(layers * 3 + layers * 2 + 2 + layers * 2) * n * n * 2,
            transcendentals=0,
        ),
    )(*args)


def _conv_core(lf, sf, o_ref, group=4):
    energies = o_ref.shape[0]
    for first in range(0, energies, group):
        last = min(first + group, energies)
        acc = [None] * (last - first)
        window = {}
        for j in range(last):
            s_row = sf[j]
            for e in range(max(first, j), last):
                if e - j not in window:
                    window[e - j] = lf[e - j]
                term = window[e - j] * s_row
                k = e - first
                acc[k] = term if acc[k] is None else acc[k] + term
            window.pop(last - 1 - j, None)
        for k in range(last - first):
            o_ref[first + k] = acc[k].astype(o_ref.dtype)


def _conv_first_kernel(x_ref, o_ref, s_out_ref, lf, sf):
    energies = o_ref.shape[0]
    h = x_ref.shape[-1] // 5
    for e in range(energies):
        lf[e, :, : 2 * h] = x_ref[e, :, : 2 * h].astype(jnp.float32)
        sf[e, :, : 2 * h] = x_ref[e, :, 2 * h : 4 * h].astype(jnp.float32)
        shared = x_ref[e, :, 4 * h :].astype(jnp.float32)
        lf[e, :, 2 * h :] = shared
        sf[e, :, 2 * h :] = pltpu.roll(shared, h // 2, 1)
    _conv_core(lf, sf, o_ref)
    s_out_ref[...] = sf[...].astype(s_out_ref.dtype)


def _conv_kernel(l_ref, s_ref, o_ref, lf, sf):
    energies = o_ref.shape[0]
    for e in range(energies):
        lf[e] = l_ref[e].astype(jnp.float32)
        sf[e] = s_ref[e].astype(jnp.float32)
    _conv_core(lf, sf, o_ref)


def _conv_call(kernel, outs, block, args):
    energies = block[0]
    elems = block[0] * block[1] * block[2]
    return pl.pallas_call(
        kernel,
        out_shape=outs,
        scratch_shapes=[pltpu.VMEM(block, jnp.float32), pltpu.VMEM(block, jnp.float32)],
        cost_estimate=pl.CostEstimate(
            flops=elems * (energies + 1), bytes_accessed=elems * 8, transcendentals=0
        ),
    )(*args)


def energy_convolve_first(x):
    energies, rows, width = x.shape
    block = (energies, rows, width // 5 * 3)
    outs = (jax.ShapeDtypeStruct(block, jnp.bfloat16), jax.ShapeDtypeStruct(block, jnp.bfloat16))
    return _conv_call(_conv_first_kernel, outs, block, (x,))


def energy_convolve(l_arr, s_arr):
    block = l_arr.shape
    return _conv_call(_conv_kernel, jax.ShapeDtypeStruct(block, jnp.bfloat16), block, (l_arr, s_arr))


def pack_symmetric(blocks):
    half = blocks.shape[-1] // 2
    rows = lax.broadcasted_iota(jnp.int32, (half, half), 0)
    cols = lax.broadcasted_iota(jnp.int32, (half, half), 1)
    top_left = blocks[:, :half, :half]
    bottom_right = blocks[:, half:, half:]
    folded = jnp.where(rows <= cols, top_left, bottom_right)
    diagonal = jnp.where(rows == cols, bottom_right, jnp.zeros_like(bottom_right))
    return jnp.concatenate([folded, blocks[:, :half, half:], diagonal], axis=-1)


def pack_screened(blocks):
    half = blocks.shape[-1] // 2
    packed = pack_symmetric(blocks)
    moved = jnp.roll(packed[..., 2 * half :], half // 2, axis=-1)
    return jnp.concatenate([packed[..., : 2 * half], moved], axis=-1)


def unpack_symmetric(packed):
    half = packed.shape[-1] // 3
    rows = lax.broadcasted_iota(jnp.int32, (half, half), 0)
    cols = lax.broadcasted_iota(jnp.int32, (half, half), 1)
    folded = packed[..., :half]
    off = packed[..., half : 2 * half]
    diagonal = packed[..., 2 * half :]
    flipped = jnp.swapaxes(folded, -1, -2)
    top_left = jnp.where(rows <= cols, folded, flipped)
    bottom_right = jnp.where(rows > cols, folded, flipped)
    bottom_right = jnp.where(rows == cols, diagonal, bottom_right)
    top = jnp.concatenate([top_left, off], axis=-1)
    bottom = jnp.concatenate([jnp.swapaxes(off, -1, -2), bottom_right], axis=-1)
    return jnp.concatenate([top, bottom], axis=-2)


def shards(retarded, scatter_in, screen):
    energies = lax.axis_size("energy")
    layers = retarded.shape[1]
    orbitals = retarded.shape[-1]
    half = orbitals // 2
    rows = layers * half // energies
    retarded = retarded[0]
    screened = symmetric(screen[0]).astype(jnp.bfloat16)

    def to_blocks(columns):
        return unpack_symmetric(columns.reshape(layers, half, columns.shape[-1]))

    scatter = scatter_in[0]
    correction = None
    screen_columns = None
    lesser = None
    self_energy = None
    for iteration in range(ITERS):
        edges = symmetric(jnp.concatenate([scatter[-1:], scatter[:1]], axis=0))
        if correction is not None:
            edge_packed = jnp.concatenate([correction[-1:], correction[:1]], axis=0)
            edges = edges + unpack_symmetric(edge_packed).astype(jnp.float32)
        edges = edges.astype(jnp.bfloat16)
        below, above = halo(jnp.concatenate([edges[1:], edges[:1]], axis=0), "layer")
        if screen_columns is None:
            lesser, both = lesser_blocks(
                retarded, scatter, None, below, above, pack_screened(screened)
            )
            both = lax.all_to_all(
                both.reshape(energies, rows, both.shape[-1]), "energy", 0, 0, tiled=True
            )
            self_columns, screen_columns = energy_convolve_first(both)
        else:
            lesser, packed = lesser_blocks(retarded, scatter, correction, below, above)
            lesser_columns = lax.all_to_all(
                packed.reshape(energies, rows, packed.shape[-1]), "energy", 0, 0, tiled=True
            )
            self_columns = energy_convolve(lesser_columns, screen_columns)
        returned = lax.all_to_all(self_columns, "energy", 0, 0, tiled=True)
        correction = returned.reshape(layers, half, returned.shape[-1])
    self_energy = to_blocks(returned)[None]
    return (lesser[None], self_energy)


def solution(mesh):
    placed = (
        P("energy", "layer", None, None, None),
        P("energy", "layer", None, None),
        P("energy", "layer", None, None),
    )
    return jax.shard_map(
        shards,
        mesh=mesh,
        in_specs=placed,
        out_specs=(P("energy", "layer", None, None), P("energy", "layer", None, None)),
        check_vma=False,
    )
```
